128 devices in a mesh: req: 8 (over y, core), exp: 16 (over z, x).
Axes of the slice: x: 4, y: 4, z: 4, core: 2. Of those that a mesh axis runs over, the one named last changes fastest.
Arguments:
- queries: bfloat16 [16, 512, 2048], P('req', None, 'exp'), may hold values from -40 to 40
- new_entries: bfloat16 [16, 2, 512, 2048], P('req', None, None, 'exp'), may hold values from -40 to 40
- cache_entries: bfloat16 [16, 2, 4096, 2048], P('req', None, None, 'exp'), may hold values from -6 to 6
- cache_lengths: int32 [16], P('req'), may hold values from 1 to 4096, 32768 in all
- out_proj: bfloat16 [2048, 2048], P('exp'), may hold values from -0.125 to 0.125
- residual: bfloat16 [8192, 2048], P(('req', 'exp')), may hold values from -40 to 40
- norm_gain: float32 [2048], replicated, may hold values from 0.1 to 1.9
- routes: int32 [8192, 8], P(('req', 'exp')), may hold values from 0 to 63, all different within a row; in each aligned block of 64 rows (0 to 63, 64 to 127, ...) at most 10 rows name the same one
- gate_weights: float32 [8192, 8], P(('req', 'exp')), may hold values from 0.1 to 0.6
- expert_in: bfloat16 [2, 2048, 65536], P(None, None, ('req', 'exp')), may hold values from -0.125 to 0.125
- expert_down: bfloat16 [65536, 2048], P(('req', 'exp')), may hold values from -0.1875 to 0.1875
Outputs:
- attended: bfloat16 [8192, 2048], P(('req', 'exp'))
- expert_out: bfloat16 [8192, 2048], P(('req', 'exp'))
The draws below stay inside these ranges and needn't reach their ends.
Inputs may be any that keep to these rules, and one draw needn't show every extreme that they name: `cache_lengths`: the lengths add up to 32768 and one is exactly 4096. `routes`: each row names 8 different experts; within the rows of one device (aligned blocks of 64 rows) no expert is named more than 10 times, a bound that some block reaches.
All inputs are finite; a program needn't handle non-finite values. No bound on the sum of `cache_lengths` on one device may be relied on, other than what follows from the above.
Results may differ from the reference program's by a relative error of at most 0.0085.
Values may be sent and summed in bfloat16 or wider, within the bound.
No kernel may reach another device: no remote copies, remote signals or barrier semaphores. Data moves between devices by JAX's collectives and lax.ppermute only.
A program may use at most 128 MiB of HBM per device.

```python
import math
import jax
import jax.numpy as jnp
import numpy as np
from jax import lax

D = 2048
HEADS = 16
HD = 128
EXPERTS = 64
FF = 1024
TOP = 8
NEW = 512
CACHE = 4096
REQUESTS = 16
TOKENS = 8192
TOK_DEV = 64
CAP = 10


def draw_queries(key, part):
    shape = (REQUESTS, NEW, HEADS, HD)
    values = jax.random.normal(jax.random.fold_in(key, 1), shape, jnp.float32)
    return values.reshape(REQUESTS, NEW, HEADS * HD).astype(jnp.bfloat16)


def draw_new_entries(key, part):
    shape = (REQUESTS, 2, NEW, HEADS, HD)
    values = jax.random.normal(jax.random.fold_in(key, 2), shape, jnp.float32)
    return values.reshape(REQUESTS, 2, NEW, HEADS * HD).astype(jnp.bfloat16)


def draw_residual(key, part):
    base = jnp.clip(jax.random.normal(jax.random.fold_in(key, 3), (TOKENS, D), jnp.float32), -4.0, 4.0)
    row_scale = jnp.exp(jax.random.uniform(jax.random.fold_in(key, 4), (TOKENS, 1), jnp.float32, math.log(0.3), math.log(3.0)))
    col_scale = jnp.exp(jax.random.uniform(jax.random.fold_in(key, 5), (1, D), jnp.float32, math.log(0.3), math.log(3.0)))
    return (base * row_scale * col_scale).astype(jnp.bfloat16)


def levels(rng, extent, pieces, smallest, high):
    gain, own = 1.0, jax.random.fold_in(rng, 6)
    for position, shards_of in pieces:
        steps = jnp.exp(jax.random.uniform(jax.random.fold_in(own, position), (shards_of,), jnp.float32, smallest / len(pieces), high / len(pieces)))
        gain = gain * jnp.repeat(steps, extent[position] // shards_of).reshape([-1 if axis == position else 1 for axis in range(len(extent))])
    return gain


def split_up(amount, total, limit, lean):
    loads = [(1 << 20) // math.isqrt(standing ** lean) + 1 for standing in range(2, amount + 1)]
    surplus, counts = total - limit - (amount - 1), [1] * (amount - 1)
    while surplus > 0:
        candidates = [i for i in range(amount - 1) if counts[i] < limit]
        pool, remaining = sum([loads[i] for i in candidates]), surplus
        for i in candidates:
            addition = min(limit - counts[i], max(1, remaining * loads[i] // pool), surplus)
            counts[i] = counts[i] + addition
            surplus = surplus - addition
    return np.array([limit] + counts)


def uneven(stream_key, number_of, total, reach, skew):
    if number_of == 2:
        one = jax.random.randint(stream_key, (), max(1, total - reach), min(reach, total - 1) + 1)
        return jnp.stack([one, total - one])
    tallies = jnp.asarray(split_up(number_of, total, reach, skew), jnp.int32)
    twos = (number_of - 1) // 2
    giver, sink = tallies[1:1 + 2 * twos:2], tallies[2:2 + 2 * twos:2]
    slack = jnp.minimum(giver - 1, reach - sink)
    passed = jax.random.randint(jax.random.fold_in(stream_key, 1), (twos,), 0, 1 << 20) % (slack + 1)
    tallies = tallies.at[1:1 + 2 * twos:2].set(giver - passed).at[2:2 + 2 * twos:2].set(sink + passed)
    return tallies[jax.random.permutation(jax.random.fold_in(stream_key, 2), number_of)]


def shared_out(key, own, number, rows, amount, top, reach, slope):
    order = jax.random.permutation(key, amount)
    crowded, common = shares(amount, rows * top, reach, slope, True), shares(amount, rows * top, reach, slope, False)
    places = jnp.arange(amount)

    def named(sizes, rotation):
        used = int((sizes > 0).sum())
        fixed = max(1, used // 4)
        shifted = fixed + (places - fixed + rotation * (used - fixed)) % max(1, amount - fixed)
        return jnp.zeros((amount,), jnp.int32).at[order[jnp.where(places < fixed, places, shifted)]].set(jnp.asarray(sizes, jnp.int32))

    sizes = jnp.where(number % 4 == 0, named(crowded, number // 4), named(common, number - number // 4 - 1))
    mixed = jax.random.permutation(jax.random.fold_in(own, 3), amount)
    source_of, taker = mixed[0:amount // 2 * 2:2], mixed[1:amount // 2 * 2:2]
    slack = jnp.minimum(sizes[source_of] - 1, reach - sizes[taker]) // 2
    slack = jnp.where((source_of == order[0]) | (taker == order[0]) | (sizes[taker] == 0), 0, jnp.maximum(slack, 0))
    shifted = jax.random.randint(jax.random.fold_in(own, 4), (amount // 2,), 0, 1 << 20) % (slack + 1)
    sizes = sizes.at[source_of].add(-shifted).at[taker].add(shifted)
    members = jnp.searchsorted(jnp.cumsum(sizes), jnp.arange(rows * top), side="right").astype(jnp.int32)
    table = members.reshape(top, rows).T
    table = table[jax.random.permutation(jax.random.fold_in(own, 1), rows)]
    rotation = jax.random.randint(jax.random.fold_in(own, 2), (rows, 1), 0, top)
    return jnp.take_along_axis(table, (jnp.arange(top)[None, :] + rotation) % top, axis=1)


def shares(count, total, most, slope, full):
    loads = [(1 << 20) // math.isqrt(standing ** slope) + 1 for standing in range(1, count + 1)]
    largest = most if full else min(most, max(-(-total // count), total * loads[0] // sum(loads)))
    least = 1 if total - largest >= count - 1 else 0
    counts, rest = [largest] + [least] * (count - 1), total - largest - least * (count - 1)
    while rest > 0:
        free = [i for i in range(1, count) if counts[i] < largest] or [i for i in range(1, count) if counts[i] < most]
        whole, budget = sum([loads[i] for i in free]), rest
        for i in free:
            addition = min(most - counts[i], max(1, budget * loads[i] // whole), rest)
            counts[i] = counts[i] + addition
            rest = rest - addition
    return np.array(counts)


def normal_values(key, dims, deviation, most, split=(), kind=jnp.bfloat16):
    factor_of = levels(key, dims, split, -0.22, 0.18) if split else 1.0
    values = jax.random.normal(key, dims, jnp.float32) * deviation * factor_of
    return jnp.minimum(jnp.maximum(values, -most), most).astype(kind)


def setup_inputs(seed: int = 0) -> dict:
    key_list = jax.random.split(jax.random.key(seed), 12)
    queries = draw_queries(jax.random.fold_in(key_list[11], 71), 0)
    new_entries = draw_new_entries(jax.random.fold_in(key_list[11], 71), 0)
    cache_entries = normal_values(key_list[2], (REQUESTS, 2, CACHE, HEADS * HD), 1.0, 6.0, ((0, 8), (3, 16)))
    cache_lengths = uneven(key_list[3], REQUESTS, REQUESTS * CACHE // 2, CACHE, 2).astype(jnp.int32)
    out_proj = normal_values(key_list[4], (HEADS * HD, D), (HEADS * HD) ** -0.5, 0.125, ((0, 16),))
    residual = draw_residual(jax.random.fold_in(key_list[11], 71), 0)
    norm_gain = jnp.clip(1.0 + 0.18 * jax.random.normal(key_list[6], (D,), jnp.float32), 0.1, 1.9)
    routes_keys = jax.random.split(jax.random.fold_in(key_list[7], 1), TOKENS // TOK_DEV)
    routes_turns = jax.random.permutation(jax.random.fold_in(key_list[7], 3), TOKENS // TOK_DEV)
    routes = jax.vmap(lambda own, number: shared_out(jax.random.fold_in(key_list[7], 2), own, number, TOK_DEV, EXPERTS, TOP, CAP, 2))(routes_keys, routes_turns).reshape((TOKENS, TOP))
    gate_weights = jnp.clip(0.1 + 0.5 * jax.random.uniform(key_list[8], (TOKENS, TOP), jnp.float32) ** levels(key_list[8], (TOKENS, TOP), ((0, 128),), -0.2, 0.2), 0.1, 0.6)
    expert_in = normal_values(key_list[9], (2, D, EXPERTS * FF), D ** -0.5, 0.125, ((2, 128),))
    expert_down = normal_values(key_list[10], (EXPERTS * FF, D), FF ** -0.5, 0.1875, ((0, 128),))
    return dict(queries=queries, new_entries=new_entries, cache_entries=cache_entries, cache_lengths=cache_lengths, out_proj=out_proj, residual=residual, norm_gain=norm_gain, routes=routes, gate_weights=gate_weights, expert_in=expert_in, expert_down=expert_down)


def attend_request(packed):
    query_rows, new_rows, cache_rows, length = packed
    query_heads = query_rows.astype(jnp.float32).reshape(NEW, HEADS, HD)
    cache_keys = cache_rows[0].astype(jnp.float32).reshape(CACHE, HEADS, HD)
    cache_vals = cache_rows[1].astype(jnp.float32).reshape(CACHE, HEADS, HD)
    new_keys = new_rows[0].astype(jnp.float32).reshape(NEW, HEADS, HD)
    new_vals = new_rows[1].astype(jnp.float32).reshape(NEW, HEADS, HD)
    scale = HD ** (-0.5)
    cache_scores = jnp.einsum('thd,jhd->htj', query_heads, cache_keys) * scale
    new_scores = jnp.einsum('thd,jhd->htj', query_heads, new_keys) * scale
    cache_valid = jnp.arange(CACHE, dtype=jnp.int32) < length
    causal = jnp.arange(NEW, dtype=jnp.int32)[None, :] <= jnp.arange(NEW, dtype=jnp.int32)[:, None]
    scores = jnp.concatenate([jnp.where(cache_valid[None, None, :], cache_scores, -1e+30), jnp.where(causal[None, :, :], new_scores, -1e+30)], axis=-1)
    peak = lax.optimization_barrier(jnp.max(scores, axis=-1, keepdims=True))
    weights = jnp.exp(scores - peak)
    denoms = lax.optimization_barrier(jnp.sum(weights, axis=-1))
    weights_bf = lax.optimization_barrier(weights.astype(jnp.bfloat16)).astype(jnp.float32)
    all_vals = jnp.concatenate([cache_vals, new_vals], axis=0)
    mixed = jnp.einsum('htj,jhd->thd', weights_bf, all_vals) / jnp.transpose(denoms)[:, :, None]
    return mixed.astype(jnp.bfloat16).reshape(NEW, HEADS * HD)

def reference(queries, new_entries, cache_entries, cache_lengths, out_proj, residual, norm_gain, routes, gate_weights, expert_in, expert_down):
    attention = lax.map(attend_request, (queries, new_entries, cache_entries, cache_lengths))
    attention = attention.reshape(TOKENS, HEADS * HD)
    hidden = residual.astype(jnp.float32) + jnp.dot(attention, out_proj, preferred_element_type=jnp.float32)
    attended = hidden.astype(jnp.bfloat16)
    mean_square = lax.optimization_barrier(jnp.mean(hidden * hidden, axis=-1, keepdims=True))
    normed = (hidden * lax.rsqrt(mean_square + 1e-05) * norm_gain).astype(jnp.bfloat16)
    assign_total = TOKENS * TOP
    blocks = TOKENS // TOK_DEV
    flat_routes = routes.reshape(assign_total).astype(jnp.int32)
    onehot = (flat_routes[:, None] == jnp.arange(EXPERTS, dtype=jnp.int32)[None, :]).astype(jnp.int32)
    onehot = onehot.reshape(blocks, TOK_DEV * TOP, EXPERTS)
    slot_index = (lax.optimization_barrier(jnp.sum(jnp.cumsum(onehot, axis=1) * onehot, axis=2)) - 1).reshape(assign_total)
    block_index = jnp.arange(assign_total, dtype=jnp.int32) // (TOK_DEV * TOP)
    positions = (block_index * CAP + slot_index).astype(jnp.int32)
    token_index = jnp.arange(assign_total, dtype=jnp.int32) // TOP
    flat_gates = gate_weights.reshape(assign_total)
    padded = jnp.concatenate([normed, jnp.zeros((1, D), jnp.bfloat16)], axis=0)
    slots_total = blocks * CAP
    half_units = FF // 2

    def one_expert(running, expert):
        chosen = flat_routes == expert
        target = jnp.where(chosen, positions, slots_total).astype(jnp.int32)
        rows_table = jnp.full((slots_total,), TOKENS, jnp.int32).at[target].set(token_index, mode='drop')
        gate_table = jnp.zeros((slots_total,), jnp.float32).at[target].set(flat_gates, mode='drop')
        rows = padded[rows_table]
        weights_in = lax.dynamic_slice_in_dim(expert_in, expert * FF, FF, 2)
        weights_down = lax.dynamic_slice_in_dim(expert_down, expert * FF, FF, 0)
        gate_part = jnp.dot(rows, weights_in[0], preferred_element_type=jnp.float32)
        up_part = jnp.dot(rows, weights_in[1], preferred_element_type=jnp.float32)
        inner = (jax.nn.silu(gate_part) * up_part).astype(jnp.bfloat16)
        first = jnp.dot(inner[:, :half_units], weights_down[:half_units], preferred_element_type=jnp.float32).astype(jnp.bfloat16)
        second = jnp.dot(inner[:, half_units:], weights_down[half_units:], preferred_element_type=jnp.float32).astype(jnp.bfloat16)
        combined = lax.optimization_barrier(first).astype(jnp.float32) + lax.optimization_barrier(second).astype(jnp.float32)
        running = running.at[rows_table].add(gate_table[:, None] * combined, mode='drop')
        return (running, None)
    totals, _ = lax.scan(one_expert, jnp.zeros((TOKENS, D), jnp.float32), jnp.arange(EXPERTS, dtype=jnp.int32))
    return (attended, totals.astype(jnp.bfloat16))
```

```python
import jax
import jax.numpy as jnp
from jax import lax
from jax.sharding import PartitionSpec as P

HD = 128
EXPERTS = 64
FF = 1024
TOP = 8


def local(
    queries,
    new_entries,
    cache_entries,
    cache_lengths,
    out_proj,
    residual,
    norm_gain,
    routes,
    gate_weights,
    expert_in,
    expert_down,
):
    req_local, new_len, width_local = queries.shape
    heads_local = width_local // HD
    cache_len = cache_entries.shape[2]
    tok_local = residual.shape[0]
    model_width = residual.shape[1]

    def attend_request(packed):
        query_rows, new_rows, cache_rows, length = packed
        query_heads = query_rows.reshape(new_len, heads_local, HD)
        cache_keys = cache_rows[0].reshape(cache_len, heads_local, HD)
        cache_vals = cache_rows[1].reshape(cache_len, heads_local, HD)
        new_keys = new_rows[0].reshape(new_len, heads_local, HD)
        new_vals = new_rows[1].reshape(new_len, heads_local, HD)
        scale = HD ** (-0.5)
        cache_scores = (
            jnp.einsum("thd,jhd->htj", query_heads, cache_keys, preferred_element_type=jnp.float32)
            * scale
        )
        new_scores = (
            jnp.einsum("thd,jhd->htj", query_heads, new_keys, preferred_element_type=jnp.float32)
            * scale
        )
        cache_valid = jnp.arange(cache_len, dtype=jnp.int32) < length
        causal = (
            jnp.arange(new_len, dtype=jnp.int32)[None, :]
            <= jnp.arange(new_len, dtype=jnp.int32)[:, None]
        )
        scores = jnp.concatenate(
            [
                jnp.where(cache_valid[None, None, :], cache_scores, -1e30),
                jnp.where(causal[None, :, :], new_scores, -1e30),
            ],
            axis=-1,
        )
        peak = jnp.max(scores, axis=-1, keepdims=True)
        weights = jnp.exp(scores - peak)
        denoms = jnp.sum(weights, axis=-1)
        weights_bf = weights.astype(jnp.bfloat16)
        all_vals = jnp.concatenate([cache_vals, new_vals], axis=0)
        mixed = jnp.einsum("htj,jhd->thd", weights_bf, all_vals, preferred_element_type=jnp.float32)
        mixed = mixed / jnp.transpose(denoms)[:, :, None]
        return mixed.astype(jnp.bfloat16).reshape(new_len, width_local)

    attention = lax.map(attend_request, (queries, new_entries, cache_entries, cache_lengths))
    attention = attention.reshape(req_local * new_len, width_local)
    projected = lax.psum_scatter(
        jnp.dot(attention, out_proj, preferred_element_type=jnp.float32).astype(jnp.bfloat16),
        "exp",
        scatter_dimension=0,
        tiled=True,
    )
    hidden = residual.astype(jnp.float32) + projected.astype(jnp.float32)
    attended = hidden.astype(jnp.bfloat16)
    mean_square = jnp.mean(hidden * hidden, axis=-1, keepdims=True)
    normed = (hidden * lax.rsqrt(mean_square + 1e-05) * norm_gain).astype(jnp.bfloat16)
    req_count = lax.axis_size("req")
    exp_count = lax.axis_size("exp")
    devices = req_count * exp_count
    half_units = FF // 2
    pieces = expert_in.shape[2] // half_units
    capacity = max(2, tok_local * TOP * 5 // (EXPERTS * 4))
    flat_routes = routes.reshape(-1)
    onehot = (flat_routes[:, None] == jnp.arange(EXPERTS, dtype=jnp.int32)[None, :]).astype(
        jnp.int32
    )
    slot_index = jnp.sum(jnp.cumsum(onehot, axis=0) * onehot, axis=1) - 1
    positions = flat_routes * capacity + slot_index
    slot_rows = (
        jnp.zeros((EXPERTS * capacity, model_width), jnp.bfloat16)
        .at[positions]
        .set(jnp.repeat(normed, TOP, axis=0))
    )
    outgoing = jnp.repeat(slot_rows.reshape(EXPERTS, capacity, model_width), 2, axis=0)
    outgoing = outgoing.reshape(devices, pieces, capacity, model_width)
    arrived = lax.all_to_all(outgoing, ("req", "exp"), split_axis=0, concat_axis=0, tiled=True)
    sources = arrived.shape[0]
    items = arrived.shape[2]
    rows = arrived[:, 0].reshape(sources * items, model_width)
    gate_part = jnp.dot(rows, expert_in[0, :, 0:half_units], preferred_element_type=jnp.float32)
    up_part = jnp.dot(rows, expert_in[1, :, 0:half_units], preferred_element_type=jnp.float32)
    inner = (jax.nn.silu(gate_part) * up_part).astype(jnp.bfloat16)
    half_out = jnp.dot(inner, expert_down, preferred_element_type=jnp.float32).astype(jnp.bfloat16)
    outputs = [half_out.reshape(sources, items, model_width)]
    returned = lax.all_to_all(
        jnp.stack(outputs, axis=1), ("req", "exp"), split_axis=0, concat_axis=0, tiled=True
    )
    halves = returned.reshape(EXPERTS, 2, capacity, model_width)
    summed = (halves[:, 0].astype(jnp.float32) + halves[:, 1].astype(jnp.float32)).reshape(
        EXPERTS * capacity, model_width
    )
    picked = summed[positions] * gate_weights.reshape(-1)[:, None]
    expert_out = jnp.sum(picked.reshape(tok_local, TOP, model_width), axis=1).astype(jnp.bfloat16)
    return (attended, expert_out)


def solution(mesh):
    return jax.shard_map(
        local,
        mesh=mesh,
        in_specs=(
            P("req", None, "exp"),
            P("req", None, None, "exp"),
            P("req", None, None, "exp"),
            P("req"),
            P("exp", None),
            P(("req", "exp"), None),
            P(),
            P(("req", "exp"), None),
            P(("req", "exp"), None),
            P(None, None, ("req", "exp")),
            P(("req", "exp"), None),
        ),
        out_specs=(P(("req", "exp"), None), P(("req", "exp"), None)),
        check_vma=False,
    )
```

```python
import jax
import jax.numpy as jnp
from jax import lax
from jax.sharding import PartitionSpec as P

HD = 128
EXPERTS = 64
FF = 1024
TOP = 8


def local(
    queries,
    new_entries,
    cache_entries,
    cache_lengths,
    out_proj,
    residual,
    norm_gain,
    routes,
    gate_weights,
    expert_in,
    expert_down,
):
    req_local, new_len, width_local = queries.shape
    heads_local = width_local // HD
    cache_len = cache_entries.shape[2]
    tok_local = residual.shape[0]
    model_width = residual.shape[1]

    def attend_request(packed):
        query_rows, new_rows, cache_rows, length = packed
        query_heads = query_rows.reshape(new_len, heads_local, HD)
        cache_keys = cache_rows[0].reshape(cache_len, heads_local, HD)
        cache_vals = cache_rows[1].reshape(cache_len, heads_local, HD)
        new_keys = new_rows[0].reshape(new_len, heads_local, HD)
        new_vals = new_rows[1].reshape(new_len, heads_local, HD)
        scale = HD ** (-0.5)
        cache_scores = (
            jnp.einsum("thd,jhd->htj", query_heads, cache_keys, preferred_element_type=jnp.float32)
            * scale
        )
        new_scores = (
            jnp.einsum("thd,jhd->htj", query_heads, new_keys, preferred_element_type=jnp.float32)
            * scale
        )
        cache_valid = jnp.arange(cache_len, dtype=jnp.int32) < length
        causal = (
            jnp.arange(new_len, dtype=jnp.int32)[None, :]
            <= jnp.arange(new_len, dtype=jnp.int32)[:, None]
        )
        scores = jnp.concatenate(
            [
                jnp.where(cache_valid[None, None, :], cache_scores, -1e30),
                jnp.where(causal[None, :, :], new_scores, -1e30),
            ],
            axis=-1,
        )
        peak = jnp.max(scores, axis=-1, keepdims=True)
        weights = jnp.exp(scores - peak)
        denoms = jnp.sum(weights, axis=-1)
        weights_bf = weights.astype(jnp.bfloat16)
        all_vals = jnp.concatenate([cache_vals, new_vals], axis=0)
        mixed = jnp.einsum("htj,jhd->thd", weights_bf, all_vals, preferred_element_type=jnp.float32)
        mixed = mixed / jnp.transpose(denoms)[:, :, None]
        return mixed.astype(jnp.bfloat16).reshape(new_len, width_local)

    attention = lax.map(attend_request, (queries, new_entries, cache_entries, cache_lengths))
    attention = attention.reshape(req_local * new_len, width_local)
    gathered = lax.all_to_all(attention, "exp", 0, 1, tiled=True)
    full_proj = lax.all_gather(out_proj, "exp", axis=0, tiled=True)
    projected = jnp.dot(gathered, full_proj, preferred_element_type=jnp.float32)
    hidden = residual.astype(jnp.float32) + projected
    attended = hidden.astype(jnp.bfloat16)
    mean_square = jnp.mean(hidden * hidden, axis=-1, keepdims=True)
    normed = (hidden * lax.rsqrt(mean_square + 1e-05) * norm_gain).astype(jnp.bfloat16)
    req_count = lax.axis_size("req")
    exp_count = lax.axis_size("exp")
    devices = req_count * exp_count
    half_units = FF // 2
    pieces = expert_in.shape[2] // half_units
    capacity = max(2, tok_local * TOP * 5 // (EXPERTS * 4))
    flat_routes = routes.reshape(-1)
    onehot = (flat_routes[:, None] == jnp.arange(EXPERTS, dtype=jnp.int32)[None, :]).astype(
        jnp.int32
    )
    slot_index = jnp.sum(jnp.cumsum(onehot, axis=0) * onehot, axis=1) - 1
    positions = flat_routes * capacity + slot_index
    slot_rows = (
        jnp.zeros((EXPERTS * capacity, model_width), jnp.bfloat16)
        .at[positions]
        .set(jnp.repeat(normed, TOP, axis=0))
    )
    outgoing = jnp.repeat(slot_rows.reshape(EXPERTS, capacity, model_width), 2, axis=0)
    outgoing = outgoing.reshape(devices, pieces, capacity, model_width)
    arrived = lax.all_to_all(outgoing, ("req", "exp"), split_axis=0, concat_axis=0, tiled=True)
    sources = arrived.shape[0]
    items = arrived.shape[2]
    rows = arrived[:, 0].reshape(sources * items, model_width)
    gate_part = jnp.dot(rows, expert_in[0, :, 0:half_units], preferred_element_type=jnp.float32)
    up_part = jnp.dot(rows, expert_in[1, :, 0:half_units], preferred_element_type=jnp.float32)
    inner = (jax.nn.silu(gate_part) * up_part).astype(jnp.bfloat16)
    half_out = jnp.dot(inner, expert_down, preferred_element_type=jnp.float32).astype(jnp.bfloat16)
    outputs = [half_out.reshape(sources, items, model_width)]
    returned = lax.all_to_all(
        jnp.stack(outputs, axis=1), ("req", "exp"), split_axis=0, concat_axis=0, tiled=True
    )
    halves = returned.reshape(EXPERTS, 2, capacity, model_width)
    summed = (halves[:, 0].astype(jnp.float32) + halves[:, 1].astype(jnp.float32)).reshape(
        EXPERTS * capacity, model_width
    )
    picked = summed[positions] * gate_weights.reshape(-1)[:, None]
    expert_out = jnp.sum(picked.reshape(tok_local, TOP, model_width), axis=1).astype(jnp.bfloat16)
    return (attended, expert_out)


def solution(mesh):
    return jax.shard_map(
        local,
        mesh=mesh,
        in_specs=(
            P("req", None, "exp"),
            P("req", None, None, "exp"),
            P("req", None, None, "exp"),
            P("req"),
            P("exp", None),
            P(("req", "exp"), None),
            P(),
            P(("req", "exp"), None),
            P(("req", "exp"), None),
            P(None, None, ("req", "exp")),
            P(("req", "exp"), None),
        ),
        out_specs=(P(("req", "exp"), None), P(("req", "exp"), None)),
        check_vma=False,
    )
```

```python
import jax
import jax.numpy as jnp
from jax import lax
from jax.sharding import PartitionSpec as P

HD = 128
EXPERTS = 64
FF = 1024
TOP = 8


def local(
    queries,
    new_entries,
    cache_entries,
    cache_lengths,
    out_proj,
    residual,
    norm_gain,
    routes,
    gate_weights,
    expert_in,
    expert_down,
):
    req_local, new_len, width_local = queries.shape
    heads_local = width_local // HD
    cache_len = cache_entries.shape[2]
    tok_local = residual.shape[0]
    model_width = residual.shape[1]

    def attend_request(packed):
        query_rows, new_rows, cache_rows, length = packed
        query_heads = query_rows.reshape(new_len, heads_local, HD)
        cache_keys = cache_rows[0].reshape(cache_len, heads_local, HD)
        cache_vals = cache_rows[1].reshape(cache_len, heads_local, HD)
        new_keys = new_rows[0].reshape(new_len, heads_local, HD)
        new_vals = new_rows[1].reshape(new_len, heads_local, HD)
        scale = HD ** (-0.5)
        cache_scores = (
            jnp.einsum("thd,jhd->htj", query_heads, cache_keys, preferred_element_type=jnp.float32)
            * scale
        )
        new_scores = (
            jnp.einsum("thd,jhd->htj", query_heads, new_keys, preferred_element_type=jnp.float32)
            * scale
        )
        cache_valid = jnp.arange(cache_len, dtype=jnp.int32) < length
        causal = (
            jnp.arange(new_len, dtype=jnp.int32)[None, :]
            <= jnp.arange(new_len, dtype=jnp.int32)[:, None]
        )
        scores = jnp.concatenate(
            [
                jnp.where(cache_valid[None, None, :], cache_scores, -1e30),
                jnp.where(causal[None, :, :], new_scores, -1e30),
            ],
            axis=-1,
        )
        peak = jnp.max(scores, axis=-1, keepdims=True)
        weights = jnp.exp(scores - peak)
        denoms = jnp.sum(weights, axis=-1)
        weights_bf = weights.astype(jnp.bfloat16)
        all_vals = jnp.concatenate([cache_vals, new_vals], axis=0)
        mixed = jnp.einsum("htj,jhd->thd", weights_bf, all_vals, preferred_element_type=jnp.float32)
        mixed = mixed / jnp.transpose(denoms)[:, :, None]
        return mixed.astype(jnp.bfloat16).reshape(new_len, width_local)

    attention = lax.map(attend_request, (queries, new_entries, cache_entries, cache_lengths))
    attention = attention.reshape(req_local * new_len, width_local)
    gathered = lax.all_to_all(attention, "exp", 0, 1, tiled=True)
    full_proj = lax.all_gather(out_proj, "exp", axis=0, tiled=True)
    projected = jnp.dot(gathered, full_proj, preferred_element_type=jnp.float32)
    hidden = residual.astype(jnp.float32) + projected
    attended = hidden.astype(jnp.bfloat16)
    mean_square = jnp.mean(hidden * hidden, axis=-1, keepdims=True)
    normed = (hidden * lax.rsqrt(mean_square + 1e-05) * norm_gain).astype(jnp.bfloat16)
    req_count = lax.axis_size("req")
    exp_count = lax.axis_size("exp")
    devices = req_count * exp_count
    half_units = FF // 2
    pieces = expert_in.shape[2] // half_units
    capacity = max(2, tok_local * TOP * 5 // (EXPERTS * 4))
    lanes = 128
    folds = model_width // lanes
    flat_routes = routes.reshape(-1)
    onehot = (flat_routes[:, None] == jnp.arange(EXPERTS, dtype=jnp.int32)[None, :]).astype(
        jnp.int32
    )
    slot_index = jnp.sum(jnp.cumsum(onehot, axis=0) * onehot, axis=1) - 1
    positions = flat_routes * capacity + slot_index
    token_of = jnp.arange(tok_local * TOP, dtype=jnp.int32) // TOP
    rows_table = jnp.full((EXPERTS * capacity,), tok_local, jnp.int32).at[positions].set(token_of)
    normed_fold = jnp.concatenate(
        [normed.reshape(tok_local, folds, lanes), jnp.zeros((1, folds, lanes), jnp.bfloat16)], axis=0
    )
    slot_rows = normed_fold[rows_table].reshape(EXPERTS, 1, capacity * folds, lanes)
    outgoing = jnp.broadcast_to(slot_rows, (EXPERTS, 2, capacity * folds, lanes))
    outgoing = outgoing.reshape(devices, pieces * capacity * folds, lanes)
    arrived = lax.all_to_all(outgoing, ("req", "exp"), 0, 0, tiled=True)
    sources = arrived.shape[0]
    rows = arrived.reshape(sources * capacity, model_width)
    gate_part = jnp.dot(rows, expert_in[0, :, 0:half_units], preferred_element_type=jnp.float32)
    up_part = jnp.dot(rows, expert_in[1, :, 0:half_units], preferred_element_type=jnp.float32)
    inner = (jax.nn.silu(gate_part) * up_part).astype(jnp.bfloat16)
    half_out = jnp.dot(inner, expert_down, preferred_element_type=jnp.float32).astype(jnp.bfloat16)
    back = half_out.reshape(sources, capacity * folds, lanes)
    returned = lax.all_to_all(back, ("req", "exp"), 0, 0, tiled=True)
    halves = returned.reshape(EXPERTS, 2, capacity, folds, lanes)
    summed = (halves[:, 0].astype(jnp.float32) + halves[:, 1].astype(jnp.float32)).reshape(
        EXPERTS * capacity, folds, lanes
    )
    picked = summed[positions] * gate_weights.reshape(-1)[:, None, None]
    expert_out = jnp.sum(picked.reshape(tok_local, TOP, folds, lanes), axis=1)
    expert_out = expert_out.astype(jnp.bfloat16).reshape(tok_local, model_width)
    return (attended, expert_out)


def solution(mesh):
    return jax.shard_map(
        local,
        mesh=mesh,
        in_specs=(
            P("req", None, "exp"),
            P("req", None, None, "exp"),
            P("req", None, None, "exp"),
            P("req"),
            P("exp", None),
            P(("req", "exp"), None),
            P(),
            P(("req", "exp"), None),
            P(("req", "exp"), None),
            P(None, None, ("req", "exp")),
            P(("req", "exp"), None),
        ),
        out_specs=(P(("req", "exp"), None), P(("req", "exp"), None)),
        check_vma=False,
    )
```

```python
import jax
import jax.numpy as jnp
from jax import lax
from jax.sharding import PartitionSpec as P

HD = 128
EXPERTS = 64
FF = 1024
TOP = 8


def local(
    queries,
    new_entries,
    cache_entries,
    cache_lengths,
    out_proj,
    residual,
    norm_gain,
    routes,
    gate_weights,
    expert_in,
    expert_down,
):
    req_local, new_len, width_local = queries.shape
    heads_local = width_local // HD
    cache_len = cache_entries.shape[2]
    tok_local = residual.shape[0]
    model_width = residual.shape[1]

    def attend_request(packed):
        query_rows, new_rows, cache_rows, length = packed
        query_heads = query_rows.reshape(new_len, heads_local, HD)
        cache_keys = cache_rows[0].reshape(cache_len, heads_local, HD)
        cache_vals = cache_rows[1].reshape(cache_len, heads_local, HD)
        new_keys = new_rows[0].reshape(new_len, heads_local, HD)
        new_vals = new_rows[1].reshape(new_len, heads_local, HD)
        scale = HD ** (-0.5)
        cache_scores = (
            jnp.einsum("thd,jhd->htj", query_heads, cache_keys, preferred_element_type=jnp.float32)
            * scale
        )
        new_scores = (
            jnp.einsum("thd,jhd->htj", query_heads, new_keys, preferred_element_type=jnp.float32)
            * scale
        )
        cache_valid = jnp.arange(cache_len, dtype=jnp.int32) < length
        causal = (
            jnp.arange(new_len, dtype=jnp.int32)[None, :]
            <= jnp.arange(new_len, dtype=jnp.int32)[:, None]
        )
        scores = jnp.concatenate(
            [
                jnp.where(cache_valid[None, None, :], cache_scores, -1e30),
                jnp.where(causal[None, :, :], new_scores, -1e30),
            ],
            axis=-1,
        )
        peak = jnp.max(scores, axis=-1, keepdims=True)
        weights = jnp.exp(scores - peak)
        denoms = jnp.sum(weights, axis=-1)
        weights_bf = weights.astype(jnp.bfloat16)
        all_vals = jnp.concatenate([cache_vals, new_vals], axis=0)
        mixed = jnp.einsum("htj,jhd->thd", weights_bf, all_vals, preferred_element_type=jnp.float32)
        mixed = mixed / jnp.transpose(denoms)[:, :, None]
        return mixed.astype(jnp.bfloat16).reshape(new_len, width_local)

    attention = lax.map(attend_request, (queries, new_entries, cache_entries, cache_lengths))
    attention = attention.reshape(req_local * new_len, width_local)
    req_count = lax.axis_size("req")
    exp_count = lax.axis_size("exp")
    share = out_proj.shape[0] // req_count
    piece = lax.dynamic_slice_in_dim(out_proj, lax.axis_index("req") * share, share, 0)
    full_proj = lax.all_gather(piece, ("req", "exp"), axis=0, tiled=True)
    gathered = lax.all_to_all(attention, "exp", 0, 1, tiled=True)
    gathered = gathered.reshape(tok_local, exp_count, req_count, share)
    gathered = jnp.transpose(gathered, (0, 2, 1, 3)).reshape(tok_local, width_local * exp_count)
    projected = jnp.dot(gathered, full_proj, preferred_element_type=jnp.float32)
    hidden = residual.astype(jnp.float32) + projected
    attended = hidden.astype(jnp.bfloat16)
    mean_square = jnp.mean(hidden * hidden, axis=-1, keepdims=True)
    normed = (hidden * lax.rsqrt(mean_square + 1e-05) * norm_gain).astype(jnp.bfloat16)
    devices = req_count * exp_count
    half_units = FF // 2
    pieces = expert_in.shape[2] // half_units
    capacity = max(2, tok_local * TOP * 5 // (EXPERTS * 4))
    lanes = 128
    folds = model_width // lanes
    flat_routes = routes.reshape(-1)
    onehot = (flat_routes[:, None] == jnp.arange(EXPERTS, dtype=jnp.int32)[None, :]).astype(
        jnp.int32
    )
    slot_index = jnp.sum(jnp.cumsum(onehot, axis=0) * onehot, axis=1) - 1
    positions = flat_routes * capacity + slot_index
    token_of = jnp.arange(tok_local * TOP, dtype=jnp.int32) // TOP
    rows_table = jnp.full((EXPERTS * capacity,), tok_local, jnp.int32).at[positions].set(token_of)
    normed_fold = jnp.concatenate(
        [normed.reshape(tok_local, folds, lanes), jnp.zeros((1, folds, lanes), jnp.bfloat16)], axis=0
    )
    slot_rows = normed_fold[rows_table].reshape(EXPERTS, 1, capacity * folds, lanes)
    outgoing = jnp.broadcast_to(slot_rows, (EXPERTS, 2, capacity * folds, lanes))
    outgoing = outgoing.reshape(devices, pieces * capacity * folds, lanes)
    arrived = lax.all_to_all(outgoing, ("req", "exp"), 0, 0, tiled=True)
    sources = arrived.shape[0]
    rows = arrived.reshape(sources * capacity, model_width)
    gate_part = jnp.dot(rows, expert_in[0, :, 0:half_units], preferred_element_type=jnp.float32)
    up_part = jnp.dot(rows, expert_in[1, :, 0:half_units], preferred_element_type=jnp.float32)
    inner = (jax.nn.silu(gate_part) * up_part).astype(jnp.bfloat16)
    half_out = jnp.dot(inner, expert_down, preferred_element_type=jnp.float32).astype(jnp.bfloat16)
    back = half_out.reshape(sources, capacity * folds, lanes)
    returned = lax.all_to_all(back, ("req", "exp"), 0, 0, tiled=True)
    halves = returned.reshape(EXPERTS, 2, capacity, folds, lanes)
    summed = (halves[:, 0].astype(jnp.float32) + halves[:, 1].astype(jnp.float32)).reshape(
        EXPERTS * capacity, folds, lanes
    )
    picked = summed[positions] * gate_weights.reshape(-1)[:, None, None]
    expert_out = jnp.sum(picked.reshape(tok_local, TOP, folds, lanes), axis=1)
    expert_out = expert_out.astype(jnp.bfloat16).reshape(tok_local, model_width)
    return (attended, expert_out)


def solution(mesh):
    return jax.shard_map(
        local,
        mesh=mesh,
        in_specs=(
            P("req", None, "exp"),
            P("req", None, None, "exp"),
            P("req", None, None, "exp"),
            P("req"),
            P("exp", None),
            P(("req", "exp"), None),
            P(),
            P(("req", "exp"), None),
            P(("req", "exp"), None),
            P(None, None, ("req", "exp")),
            P(("req", "exp"), None),
        ),
        out_specs=(P(("req", "exp"), None), P(("req", "exp"), None)),
        check_vma=False,
    )
```

```python
import jax
import jax.numpy as jnp
from jax import lax
from jax.sharding import PartitionSpec as P

HD = 128
EXPERTS = 64
FF = 1024
TOP = 8


def local(
    queries,
    new_entries,
    cache_entries,
    cache_lengths,
    out_proj,
    residual,
    norm_gain,
    routes,
    gate_weights,
    expert_in,
    expert_down,
):
    req_local, new_len, width_local = queries.shape
    heads_local = width_local // HD
    cache_len = cache_entries.shape[2]
    tok_local = residual.shape[0]
    model_width = residual.shape[1]

    def attend_request(packed):
        query_rows, new_rows, cache_rows, length = packed
        query_heads = query_rows.reshape(new_len, heads_local, HD)
        cache_keys = cache_rows[0].reshape(cache_len, heads_local, HD)
        cache_vals = cache_rows[1].reshape(cache_len, heads_local, HD)
        new_keys = new_rows[0].reshape(new_len, heads_local, HD)
        new_vals = new_rows[1].reshape(new_len, heads_local, HD)
        scale = HD ** (-0.5)
        cache_scores = (
            jnp.einsum("thd,jhd->htj", query_heads, cache_keys, preferred_element_type=jnp.float32)
            * scale
        )
        new_scores = (
            jnp.einsum("thd,jhd->htj", query_heads, new_keys, preferred_element_type=jnp.float32)
            * scale
        )
        cache_valid = jnp.arange(cache_len, dtype=jnp.int32) < length
        causal = (
            jnp.arange(new_len, dtype=jnp.int32)[None, :]
            <= jnp.arange(new_len, dtype=jnp.int32)[:, None]
        )
        scores = jnp.concatenate(
            [
                jnp.where(cache_valid[None, None, :], cache_scores, -1e30),
                jnp.where(causal[None, :, :], new_scores, -1e30),
            ],
            axis=-1,
        )
        peak = jnp.max(scores, axis=-1, keepdims=True)
        weights = jnp.exp(scores - peak)
        denoms = jnp.sum(weights, axis=-1)
        weights_bf = weights.astype(jnp.bfloat16)
        all_vals = jnp.concatenate([cache_vals, new_vals], axis=0)
        mixed = jnp.einsum("htj,jhd->thd", weights_bf, all_vals, preferred_element_type=jnp.float32)
        mixed = mixed / jnp.transpose(denoms)[:, :, None]
        return mixed.astype(jnp.bfloat16).reshape(new_len, width_local)

    attention = lax.map(attend_request, (queries, new_entries, cache_entries, cache_lengths))
    attention = attention.reshape(req_local * new_len, width_local)
    req_count = lax.axis_size("req")
    exp_count = lax.axis_size("exp")
    share = out_proj.shape[0] // req_count
    piece = lax.dynamic_slice_in_dim(out_proj, lax.axis_index("req") * share, share, 0)
    full_proj = lax.all_gather(piece, ("req", "exp"), axis=0, tiled=True)
    gathered = lax.all_to_all(attention, "exp", 0, 1, tiled=True)
    gathered = gathered.reshape(tok_local, exp_count, req_count, share)
    gathered = jnp.transpose(gathered, (0, 2, 1, 3)).reshape(tok_local, width_local * exp_count)
    projected = jnp.dot(gathered, full_proj, preferred_element_type=jnp.float32)
    hidden = residual.astype(jnp.float32) + projected
    attended = hidden.astype(jnp.bfloat16)
    mean_square = jnp.mean(hidden * hidden, axis=-1, keepdims=True)
    normed = (hidden * lax.rsqrt(mean_square + 1e-05) * norm_gain).astype(jnp.bfloat16)
    devices = req_count * exp_count
    half_units = FF // 2
    pieces = expert_in.shape[2] // half_units
    capacity = max(2, tok_local * TOP * 5 // (EXPERTS * 4))
    lanes = 128
    folds = model_width // lanes
    flat_routes = routes.reshape(-1)
    onehot = (flat_routes[:, None] == jnp.arange(EXPERTS, dtype=jnp.int32)[None, :]).astype(
        jnp.int32
    )
    slot_index = jnp.sum(jnp.cumsum(onehot, axis=0) * onehot, axis=1) - 1
    positions = flat_routes * capacity + slot_index
    token_of = jnp.arange(tok_local * TOP, dtype=jnp.int32) // TOP
    rows_table = jnp.full((EXPERTS * capacity,), tok_local, jnp.int32).at[positions].set(token_of)
    normed_fold = jnp.concatenate(
        [normed.reshape(tok_local, folds, lanes), jnp.zeros((1, folds, lanes), jnp.bfloat16)], axis=0
    )
    slot_rows = normed_fold[rows_table].reshape(EXPERTS, 1, capacity, folds, lanes)
    chunks = 2
    fold_chunk = folds // chunks
    width_chunk = fold_chunk * lanes
    gate_part = 0.0
    up_part = 0.0
    for c in range(chunks):
        part = slot_rows[:, :, :, c * fold_chunk : (c + 1) * fold_chunk, :]
        outgoing = jnp.broadcast_to(part, (EXPERTS, 2, capacity, fold_chunk, lanes))
        outgoing = outgoing.reshape(devices, pieces * capacity * fold_chunk, lanes)
        arrived = lax.all_to_all(outgoing, ("req", "exp"), 0, 0, tiled=True)
        sources = arrived.shape[0]
        rows = arrived.reshape(sources * capacity, width_chunk)
        cols = slice(c * width_chunk, (c + 1) * width_chunk)
        gate_part = gate_part + jnp.dot(
            rows, expert_in[0, cols, 0:half_units], preferred_element_type=jnp.float32
        )
        up_part = up_part + jnp.dot(
            rows, expert_in[1, cols, 0:half_units], preferred_element_type=jnp.float32
        )
    inner = (jax.nn.silu(gate_part) * up_part).astype(jnp.bfloat16)
    gates = gate_weights.reshape(-1)[:, None, None]
    outs = []
    for c in range(chunks):
        cols = slice(c * width_chunk, (c + 1) * width_chunk)
        half_out = jnp.dot(
            inner, expert_down[:, cols], preferred_element_type=jnp.float32
        ).astype(jnp.bfloat16)
        back = half_out.reshape(sources, capacity * fold_chunk, lanes)
        returned = lax.all_to_all(back, ("req", "exp"), 0, 0, tiled=True)
        halves = returned.reshape(EXPERTS, 2, capacity, fold_chunk, lanes)
        summed = (halves[:, 0].astype(jnp.float32) + halves[:, 1].astype(jnp.float32)).reshape(
            EXPERTS * capacity, fold_chunk, lanes
        )
        picked = summed[positions] * gates
        outs.append(jnp.sum(picked.reshape(tok_local, TOP, fold_chunk, lanes), axis=1))
    expert_out = jnp.concatenate(outs, axis=1)
    expert_out = expert_out.astype(jnp.bfloat16).reshape(tok_local, model_width)
    return (attended, expert_out)


def solution(mesh):
    return jax.shard_map(
        local,
        mesh=mesh,
        in_specs=(
            P("req", None, "exp"),
            P("req", None, None, "exp"),
            P("req", None, None, "exp"),
            P("req"),
            P("exp", None),
            P(("req", "exp"), None),
            P(),
            P(("req", "exp"), None),
            P(("req", "exp"), None),
            P(None, None, ("req", "exp")),
            P(("req", "exp"), None),
        ),
        out_specs=(P(("req", "exp"), None), P(("req", "exp"), None)),
        check_vma=False,
    )
```

```python
import jax
import jax.numpy as jnp
from jax import lax
from jax.sharding import Mesh, PartitionSpec as P


HD = 128
EXPERTS = 64
FF = 1024
TOP = 8


def layer(
    queries,
    new_entries,
    cache_entries,
    cache_lengths,
    out_proj,
    residual,
    norm_gain,
    routes,
    gate_weights,
    expert_in,
    expert_down,
):
    req_local, new_len, width_local = queries.shape
    heads_local = width_local // HD
    cache_len = cache_entries.shape[2]
    tok_local = residual.shape[0]
    model_width = residual.shape[1]

    def attend_request(packed):
        query_rows, new_rows, cache_rows, length = packed
        query_heads = query_rows.reshape(new_len, heads_local, HD)
        cache_keys = cache_rows[0].reshape(cache_len, heads_local, HD)
        cache_vals = cache_rows[1].reshape(cache_len, heads_local, HD)
        new_keys = new_rows[0].reshape(new_len, heads_local, HD)
        new_vals = new_rows[1].reshape(new_len, heads_local, HD)
        scale = HD ** (-0.5)
        cache_scores = (
            jnp.einsum("thd,jhd->htj", query_heads, cache_keys, preferred_element_type=jnp.float32)
            * scale
        )
        new_scores = (
            jnp.einsum("thd,jhd->htj", query_heads, new_keys, preferred_element_type=jnp.float32)
            * scale
        )
        cache_valid = jnp.arange(cache_len, dtype=jnp.int32) < length
        causal = (
            jnp.arange(new_len, dtype=jnp.int32)[None, :]
            <= jnp.arange(new_len, dtype=jnp.int32)[:, None]
        )
        scores = jnp.concatenate(
            [
                jnp.where(cache_valid[None, None, :], cache_scores, -1e30),
                jnp.where(causal[None, :, :], new_scores, -1e30),
            ],
            axis=-1,
        )
        peak = jnp.max(scores, axis=-1, keepdims=True)
        weights = jnp.exp(scores - peak)
        denoms = jnp.sum(weights, axis=-1)
        weights_bf = weights.astype(jnp.bfloat16)
        all_vals = jnp.concatenate([cache_vals, new_vals], axis=0)
        mixed = jnp.einsum("htj,jhd->thd", weights_bf, all_vals, preferred_element_type=jnp.float32)
        mixed = mixed / jnp.transpose(denoms)[:, :, None]
        return mixed.astype(jnp.bfloat16).reshape(new_len, width_local)

    attention = lax.map(attend_request, (queries, new_entries, cache_entries, cache_lengths))
    attention = attention.reshape(req_local * new_len, width_local)
    req_count = lax.axis_size("req")
    z_count = lax.axis_size("z")
    x_count = lax.axis_size("x")
    x_here = lax.axis_index("x")
    shifted = [out_proj]
    for step in range(1, x_count):
        pairs = [(i, (i + step) % x_count) for i in range(x_count)]
        shifted.append(lax.ppermute(out_proj, "x", pairs))
    stacked = jnp.stack(shifted)
    order = (x_here - jnp.arange(x_count, dtype=jnp.int32)) % x_count
    row_proj = stacked[order]
    row_proj = row_proj.reshape(x_count * width_local, model_width)
    rows_att = attention.reshape(z_count, x_count, tok_local, width_local)
    rows_att = jnp.transpose(rows_att, (1, 0, 2, 3))
    rows_att = lax.all_to_all(rows_att, "x", 0, 0, tiled=True)
    rows_att = jnp.transpose(rows_att, (1, 2, 0, 3)).reshape(
        z_count * tok_local, x_count * width_local
    )
    partial = jnp.dot(rows_att, row_proj, preferred_element_type=jnp.float32)
    partial = partial.reshape(z_count, tok_local, model_width)
    partial = lax.all_to_all(partial, "z", 0, 0, tiled=True)
    projected = jnp.sum(partial, axis=0)
    hidden = residual.astype(jnp.float32) + projected
    attended = hidden.astype(jnp.bfloat16)
    mean_square = jnp.mean(hidden * hidden, axis=-1, keepdims=True)
    normed = (hidden * lax.rsqrt(mean_square + 1e-05) * norm_gain).astype(jnp.bfloat16)
    devices = req_count * z_count * x_count
    half_units = FF // 2
    pieces = expert_in.shape[2] // half_units
    capacity = max(2, tok_local * TOP * 5 // (EXPERTS * 4))
    lanes = 128
    folds = model_width // lanes
    flat_routes = routes.reshape(-1)
    onehot = (flat_routes[:, None] == jnp.arange(EXPERTS, dtype=jnp.int32)[None, :]).astype(
        jnp.int32
    )
    slot_index = jnp.sum(jnp.cumsum(onehot, axis=0) * onehot, axis=1) - 1
    positions = flat_routes * capacity + slot_index
    token_of = jnp.arange(tok_local * TOP, dtype=jnp.int32) // TOP
    rows_table = jnp.full((EXPERTS * capacity,), tok_local, jnp.int32).at[positions].set(token_of)
    normed_fold = jnp.concatenate(
        [normed.reshape(tok_local, folds, lanes), jnp.zeros((1, folds, lanes), jnp.bfloat16)], axis=0
    )
    slot_rows = normed_fold[rows_table].reshape(EXPERTS, 1, capacity * folds, lanes)
    outgoing = jnp.broadcast_to(slot_rows, (EXPERTS, 2, capacity * folds, lanes))
    outgoing = outgoing.reshape(devices, pieces * capacity * folds, lanes)
    arrived = lax.all_to_all(outgoing, ("req", "z", "x"), 0, 0, tiled=True)
    sources = arrived.shape[0]
    rows = arrived.reshape(sources * capacity, model_width)
    gate_part = jnp.dot(rows, expert_in[0, :, 0:half_units], preferred_element_type=jnp.float32)
    up_part = jnp.dot(rows, expert_in[1, :, 0:half_units], preferred_element_type=jnp.float32)
    inner = (jax.nn.silu(gate_part) * up_part).astype(jnp.bfloat16)
    half_out = jnp.dot(inner, expert_down, preferred_element_type=jnp.float32).astype(jnp.bfloat16)
    back = half_out.reshape(sources, capacity * folds, lanes)
    returned = lax.all_to_all(back, ("req", "z", "x"), 0, 0, tiled=True)
    halves = returned.reshape(EXPERTS, 2, capacity, folds, lanes)
    summed = (halves[:, 0].astype(jnp.float32) + halves[:, 1].astype(jnp.float32)).reshape(
        EXPERTS * capacity, folds, lanes
    )
    picked = summed[positions] * gate_weights.reshape(-1)[:, None, None]
    expert_out = jnp.sum(picked.reshape(tok_local, TOP, folds, lanes), axis=1)
    expert_out = expert_out.astype(jnp.bfloat16).reshape(tok_local, model_width)
    return (attended, expert_out)


def solution(mesh):
    req_size, exp_size = mesh.devices.shape
    x_size = 4 if exp_size % 4 == 0 else 1
    sub_mesh = Mesh(
        mesh.devices.reshape(req_size, exp_size // x_size, x_size), ("req", "z", "x")
    )
    exp = ("z", "x")
    flat = ("req", "z", "x")
    return jax.shard_map(
        layer,
        mesh=sub_mesh,
        in_specs=(
            P("req", None, exp),
            P("req", None, None, exp),
            P("req", None, None, exp),
            P("req"),
            P(exp, None),
            P(flat, None),
            P(),
            P(flat, None),
            P(flat, None),
            P(None, None, flat),
            P(flat, None),
        ),
        out_specs=(P(flat, None), P(flat, None)),
        check_vma=False,
    )
```

```python
import jax
import jax.numpy as jnp
from jax import lax
from jax.sharding import Mesh, PartitionSpec as P


HD = 128
EXPERTS = 64
FF = 1024
TOP = 8


def layer(
    queries,
    new_entries,
    cache_entries,
    cache_lengths,
    out_proj,
    residual,
    norm_gain,
    routes,
    gate_weights,
    expert_in,
    expert_down,
):
    req_local, new_len, width_local = queries.shape
    heads_local = width_local // HD
    cache_len = cache_entries.shape[2]
    tok_local = residual.shape[0]
    model_width = residual.shape[1]

    def attend_request(packed):
        query_rows, new_rows, cache_rows, length = packed
        query_heads = query_rows.reshape(new_len, heads_local, HD)
        cache_keys = cache_rows[0].reshape(cache_len, heads_local, HD)
        cache_vals = cache_rows[1].reshape(cache_len, heads_local, HD)
        new_keys = new_rows[0].reshape(new_len, heads_local, HD)
        new_vals = new_rows[1].reshape(new_len, heads_local, HD)
        scale = HD ** (-0.5)
        cache_scores = (
            jnp.einsum("thd,jhd->htj", query_heads, cache_keys, preferred_element_type=jnp.float32)
            * scale
        )
        new_scores = (
            jnp.einsum("thd,jhd->htj", query_heads, new_keys, preferred_element_type=jnp.float32)
            * scale
        )
        cache_valid = jnp.arange(cache_len, dtype=jnp.int32) < length
        causal = (
            jnp.arange(new_len, dtype=jnp.int32)[None, :]
            <= jnp.arange(new_len, dtype=jnp.int32)[:, None]
        )
        scores = jnp.concatenate(
            [
                jnp.where(cache_valid[None, None, :], cache_scores, -1e30),
                jnp.where(causal[None, :, :], new_scores, -1e30),
            ],
            axis=-1,
        )
        peak = jnp.max(scores, axis=-1, keepdims=True)
        weights = jnp.exp(scores - peak)
        denoms = jnp.sum(weights, axis=-1)
        weights_bf = weights.astype(jnp.bfloat16)
        all_vals = jnp.concatenate([cache_vals, new_vals], axis=0)
        mixed = jnp.einsum("htj,jhd->thd", weights_bf, all_vals, preferred_element_type=jnp.float32)
        mixed = mixed / jnp.transpose(denoms)[:, :, None]
        return mixed.astype(jnp.bfloat16).reshape(new_len, width_local)

    attention = lax.map(attend_request, (queries, new_entries, cache_entries, cache_lengths))
    attention = attention.reshape(req_local * new_len, width_local)
    req_count = lax.axis_size("req")
    z_count = lax.axis_size("z")
    x_count = lax.axis_size("x")
    x_here = lax.axis_index("x")
    shifted = [out_proj]
    for step in range(1, x_count):
        pairs = [(i, (i + step) % x_count) for i in range(x_count)]
        shifted.append(lax.ppermute(out_proj, "x", pairs))
    row_proj = jnp.stack(shifted)
    row_proj = row_proj.reshape(x_count * width_local, model_width)
    rows_att = attention.reshape(z_count, x_count, tok_local, width_local)
    rows_att = jnp.transpose(rows_att, (1, 0, 2, 3))
    rows_att = lax.all_to_all(rows_att, "x", 0, 0, tiled=True)
    order = (x_here - jnp.arange(x_count, dtype=jnp.int32)) % x_count
    rows_att = rows_att[order]
    rows_att = jnp.transpose(rows_att, (1, 2, 0, 3)).reshape(
        z_count * tok_local, x_count * width_local
    )
    partial = jnp.dot(rows_att, row_proj, preferred_element_type=jnp.float32)
    partial = partial.astype(jnp.bfloat16).reshape(z_count, tok_local, model_width)
    partial = lax.all_to_all(partial, "z", 0, 0, tiled=True)
    projected = jnp.sum(partial.astype(jnp.float32), axis=0)
    hidden = residual.astype(jnp.float32) + projected
    attended = hidden.astype(jnp.bfloat16)
    mean_square = jnp.mean(hidden * hidden, axis=-1, keepdims=True)
    normed = (hidden * lax.rsqrt(mean_square + 1e-05) * norm_gain).astype(jnp.bfloat16)
    devices = req_count * z_count * x_count
    half_units = FF // 2
    pieces = expert_in.shape[2] // half_units
    capacity = max(2, tok_local * TOP * 5 // (EXPERTS * 4))
    lanes = 128
    folds = model_width // lanes
    flat_routes = routes.reshape(-1)
    onehot = (flat_routes[:, None] == jnp.arange(EXPERTS, dtype=jnp.int32)[None, :]).astype(
        jnp.int32
    )
    slot_index = jnp.sum(jnp.cumsum(onehot, axis=0) * onehot, axis=1) - 1
    positions = flat_routes * capacity + slot_index
    token_of = jnp.arange(tok_local * TOP, dtype=jnp.int32) // TOP
    rows_table = jnp.full((EXPERTS * capacity,), tok_local, jnp.int32).at[positions].set(token_of)
    normed_fold = jnp.concatenate(
        [normed.reshape(tok_local, folds, lanes), jnp.zeros((1, folds, lanes), jnp.bfloat16)], axis=0
    )
    slot_rows = normed_fold[rows_table].reshape(EXPERTS, 1, capacity * folds, lanes)
    outgoing = jnp.broadcast_to(slot_rows, (EXPERTS, 2, capacity * folds, lanes))
    outgoing = outgoing.reshape(devices, pieces * capacity * folds, lanes)
    arrived = lax.all_to_all(outgoing, ("req", "z", "x"), 0, 0, tiled=True)
    sources = arrived.shape[0]
    rows = arrived.reshape(sources * capacity, model_width)
    gate_part = jnp.dot(rows, expert_in[0, :, 0:half_units], preferred_element_type=jnp.float32)
    up_part = jnp.dot(rows, expert_in[1, :, 0:half_units], preferred_element_type=jnp.float32)
    inner = (jax.nn.silu(gate_part) * up_part).astype(jnp.bfloat16)
    half_out = jnp.dot(inner, expert_down, preferred_element_type=jnp.float32).astype(jnp.bfloat16)
    back = half_out.reshape(sources, capacity * folds, lanes)
    returned = lax.all_to_all(back, ("req", "z", "x"), 0, 0, tiled=True)
    halves = returned.reshape(EXPERTS, 2, capacity, folds, lanes)
    summed = (halves[:, 0].astype(jnp.float32) + halves[:, 1].astype(jnp.float32)).reshape(
        EXPERTS * capacity, folds, lanes
    )
    picked = summed[positions] * gate_weights.reshape(-1)[:, None, None]
    expert_out = jnp.sum(picked.reshape(tok_local, TOP, folds, lanes), axis=1)
    expert_out = expert_out.astype(jnp.bfloat16).reshape(tok_local, model_width)
    return (attended, expert_out)


def solution(mesh):
    req_size, exp_size = mesh.devices.shape
    x_size = 4 if exp_size % 4 == 0 else 1
    sub_mesh = Mesh(
        mesh.devices.reshape(req_size, exp_size // x_size, x_size), ("req", "z", "x")
    )
    exp = ("z", "x")
    flat = ("req", "z", "x")
    return jax.shard_map(
        layer,
        mesh=sub_mesh,
        in_specs=(
            P("req", None, exp),
            P("req", None, None, exp),
            P("req", None, None, exp),
            P("req"),
            P(exp, None),
            P(flat, None),
            P(),
            P(flat, None),
            P(flat, None),
            P(None, None, flat),
            P(flat, None),
        ),
        out_specs=(P(flat, None), P(flat, None)),
        check_vma=False,
    )
```

```python
import jax
import jax.numpy as jnp
from jax import lax
from jax.sharding import Mesh, PartitionSpec as P


HD = 128
EXPERTS = 64
FF = 1024
TOP = 8


def layer(
    queries,
    new_entries,
    cache_entries,
    cache_lengths,
    out_proj,
    residual,
    norm_gain,
    routes,
    gate_weights,
    expert_in,
    expert_down,
):
    req_local, new_len, width_local = queries.shape
    heads_local = width_local // HD
    cache_len = cache_entries.shape[2]
    tok_local = residual.shape[0]
    model_width = residual.shape[1]

    def attend_request(packed):
        query_rows, new_rows, cache_rows, length = packed
        query_heads = query_rows.reshape(new_len, heads_local, HD)
        cache_keys = cache_rows[0].reshape(cache_len, heads_local, HD)
        cache_vals = cache_rows[1].reshape(cache_len, heads_local, HD)
        new_keys = new_rows[0].reshape(new_len, heads_local, HD)
        new_vals = new_rows[1].reshape(new_len, heads_local, HD)
        scale = HD ** (-0.5)
        cache_scores = (
            jnp.einsum("thd,jhd->htj", query_heads, cache_keys, preferred_element_type=jnp.float32)
            * scale
        )
        new_scores = (
            jnp.einsum("thd,jhd->htj", query_heads, new_keys, preferred_element_type=jnp.float32)
            * scale
        )
        cache_valid = jnp.arange(cache_len, dtype=jnp.int32) < length
        causal = (
            jnp.arange(new_len, dtype=jnp.int32)[None, :]
            <= jnp.arange(new_len, dtype=jnp.int32)[:, None]
        )
        scores = jnp.concatenate(
            [
                jnp.where(cache_valid[None, None, :], cache_scores, -1e30),
                jnp.where(causal[None, :, :], new_scores, -1e30),
            ],
            axis=-1,
        )
        peak = jnp.max(scores, axis=-1, keepdims=True)
        weights = jnp.exp(scores - peak)
        denoms = jnp.sum(weights, axis=-1)
        weights_bf = weights.astype(jnp.bfloat16)
        all_vals = jnp.concatenate([cache_vals, new_vals], axis=0)
        mixed = jnp.einsum("htj,jhd->thd", weights_bf, all_vals, preferred_element_type=jnp.float32)
        mixed = mixed / jnp.transpose(denoms)[:, :, None]
        return mixed.astype(jnp.bfloat16).reshape(new_len, width_local)

    attention = lax.map(attend_request, (queries, new_entries, cache_entries, cache_lengths))
    attention = attention.reshape(req_local * new_len, width_local)
    req_count = lax.axis_size("req")
    z_count = lax.axis_size("z")
    x_count = lax.axis_size("x")
    x_here = lax.axis_index("x")
    shifted = [out_proj]
    for step in range(1, x_count):
        pairs = [(i, (i + step) % x_count) for i in range(x_count)]
        shifted.append(lax.ppermute(out_proj, "x", pairs))
    row_proj = jnp.stack(shifted)
    row_proj = row_proj.reshape(x_count * width_local, model_width)
    rows_att = attention.reshape(z_count, x_count, tok_local, width_local)
    rows_att = jnp.transpose(rows_att, (1, 0, 2, 3))
    rows_att = lax.all_to_all(rows_att, "x", 0, 0, tiled=True)
    order = (x_here - jnp.arange(x_count, dtype=jnp.int32)) % x_count
    rows_att = rows_att[order]
    rows_att = jnp.transpose(rows_att, (1, 2, 0, 3)).reshape(
        z_count * tok_local, x_count * width_local
    )
    partial = jnp.dot(rows_att, row_proj, preferred_element_type=jnp.float32)
    partial = partial.astype(jnp.bfloat16).reshape(z_count, tok_local, model_width)
    partial = lax.all_to_all(partial, "z", 0, 0, tiled=True)
    projected = jnp.sum(partial.astype(jnp.float32), axis=0)
    hidden = residual.astype(jnp.float32) + projected
    attended = hidden.astype(jnp.bfloat16)
    mean_square = jnp.mean(hidden * hidden, axis=-1, keepdims=True)
    normed = (hidden * lax.rsqrt(mean_square + 1e-05) * norm_gain).astype(jnp.bfloat16)
    devices = req_count * z_count * x_count
    half_units = FF // 2
    pieces = expert_in.shape[2] // half_units
    capacity = max(2, tok_local * TOP * 5 // (EXPERTS * 4))
    lanes = 128
    folds = model_width // lanes
    flat_routes = routes.reshape(-1)
    onehot = (flat_routes[:, None] == jnp.arange(EXPERTS, dtype=jnp.int32)[None, :]).astype(
        jnp.int32
    )
    slot_index = jnp.sum(jnp.cumsum(onehot, axis=0) * onehot, axis=1) - 1
    positions = flat_routes * capacity + slot_index
    token_of = jnp.arange(tok_local * TOP, dtype=jnp.int32) // TOP
    rows_table = jnp.full((EXPERTS * capacity,), tok_local, jnp.int32).at[positions].set(token_of)
    normed_fold = jnp.concatenate(
        [normed.reshape(tok_local, folds, lanes), jnp.zeros((1, folds, lanes), jnp.bfloat16)], axis=0
    )
    slot_rows = normed_fold[rows_table].reshape(EXPERTS, 1, capacity * folds, lanes)
    outgoing = jnp.broadcast_to(slot_rows, (EXPERTS, 2, capacity * folds, lanes))
    outgoing = outgoing.reshape(devices, pieces * capacity * folds, lanes)
    arrived = lax.all_to_all(outgoing, ("req", "z", "x"), 0, 0, tiled=True)
    sources = arrived.shape[0]
    rows = arrived.reshape(sources * capacity, folds, lanes)
    w_in = expert_in[:, :, 0:half_units].reshape(2, folds, lanes, half_units)
    gate_part = jnp.einsum("tkd,kdf->tf", rows, w_in[0], preferred_element_type=jnp.float32)
    up_part = jnp.einsum("tkd,kdf->tf", rows, w_in[1], preferred_element_type=jnp.float32)
    inner = (jax.nn.silu(gate_part) * up_part).astype(jnp.bfloat16)
    w_down = expert_down.reshape(half_units, folds, lanes)
    half_out = jnp.einsum(
        "tf,fkd->tkd", inner, w_down, preferred_element_type=jnp.float32
    ).astype(jnp.bfloat16)
    back = half_out.reshape(sources, capacity * folds, lanes)
    returned = lax.all_to_all(back, ("req", "z", "x"), 0, 0, tiled=True)
    halves = returned.reshape(EXPERTS, 2, capacity, folds, lanes)
    summed = (halves[:, 0].astype(jnp.float32) + halves[:, 1].astype(jnp.float32)).reshape(
        EXPERTS * capacity, folds, lanes
    )
    picked = summed[positions] * gate_weights.reshape(-1)[:, None, None]
    expert_out = jnp.sum(picked.reshape(tok_local, TOP, folds, lanes), axis=1)
    expert_out = expert_out.astype(jnp.bfloat16).reshape(tok_local, model_width)
    return (attended, expert_out)


def solution(mesh):
    req_size, exp_size = mesh.devices.shape
    x_size = 4 if exp_size % 4 == 0 else 1
    sub_mesh = Mesh(
        mesh.devices.reshape(req_size, exp_size // x_size, x_size), ("req", "z", "x")
    )
    exp = ("z", "x")
    flat = ("req", "z", "x")
    return jax.shard_map(
        layer,
        mesh=sub_mesh,
        in_specs=(
            P("req", None, exp),
            P("req", None, None, exp),
            P("req", None, None, exp),
            P("req"),
            P(exp, None),
            P(flat, None),
            P(),
            P(flat, None),
            P(flat, None),
            P(None, None, flat),
            P(flat, None),
        ),
        out_specs=(P(flat, None), P(flat, None)),
        check_vma=False,
    )
```

```python
import jax
import jax.numpy as jnp
from jax import lax
from jax.sharding import Mesh, PartitionSpec as P


HD = 128
EXPERTS = 64
FF = 1024
TOP = 8


def layer(
    queries,
    new_entries,
    cache_entries,
    cache_lengths,
    out_proj,
    residual,
    norm_gain,
    routes,
    gate_weights,
    expert_in,
    expert_down,
):
    req_local, new_len, width_local = queries.shape
    heads_local = width_local // HD
    cache_len = cache_entries.shape[2]
    tok_local = residual.shape[0]
    model_width = residual.shape[1]

    def attend_request(packed):
        query_rows, new_rows, cache_rows, length = packed
        query_heads = query_rows.reshape(new_len, heads_local, HD)
        cache_keys = cache_rows[0].reshape(cache_len, heads_local, HD)
        cache_vals = cache_rows[1].reshape(cache_len, heads_local, HD)
        new_keys = new_rows[0].reshape(new_len, heads_local, HD)
        new_vals = new_rows[1].reshape(new_len, heads_local, HD)
        scale = HD ** (-0.5)
        cache_scores = (
            jnp.einsum("thd,jhd->htj", query_heads, cache_keys, preferred_element_type=jnp.float32)
            * scale
        )
        new_scores = (
            jnp.einsum("thd,jhd->htj", query_heads, new_keys, preferred_element_type=jnp.float32)
            * scale
        )
        cache_valid = jnp.arange(cache_len, dtype=jnp.int32) < length
        causal = (
            jnp.arange(new_len, dtype=jnp.int32)[None, :]
            <= jnp.arange(new_len, dtype=jnp.int32)[:, None]
        )
        scores = jnp.concatenate(
            [
                jnp.where(cache_valid[None, None, :], cache_scores, -1e30),
                jnp.where(causal[None, :, :], new_scores, -1e30),
            ],
            axis=-1,
        )
        peak = jnp.max(scores, axis=-1, keepdims=True)
        weights = jnp.exp(scores - peak)
        denoms = jnp.sum(weights, axis=-1)
        weights_bf = weights.astype(jnp.bfloat16)
        all_vals = jnp.concatenate([cache_vals, new_vals], axis=0)
        mixed = jnp.einsum("htj,jhd->thd", weights_bf, all_vals, preferred_element_type=jnp.float32)
        mixed = mixed / jnp.transpose(denoms)[:, :, None]
        return mixed.astype(jnp.bfloat16).reshape(new_len, width_local)

    attention = lax.map(attend_request, (queries, new_entries, cache_entries, cache_lengths))
    attention = attention.reshape(req_local * new_len, width_local)
    req_count = lax.axis_size("req")
    z_count = lax.axis_size("z")
    x_count = lax.axis_size("x")
    x_here = lax.axis_index("x")
    shifted = [out_proj]
    for step in range(1, x_count):
        pairs = [(i, (i + step) % x_count) for i in range(x_count)]
        shifted.append(lax.ppermute(out_proj, "x", pairs))
    row_proj = jnp.stack(shifted)
    row_proj = row_proj.reshape(x_count * width_local, model_width)
    rows_att = attention.reshape(z_count, x_count, tok_local, width_local)
    rows_att = jnp.transpose(rows_att, (1, 0, 2, 3))
    rows_att = lax.all_to_all(rows_att, "x", 0, 0, tiled=True)
    order = (x_here - jnp.arange(x_count, dtype=jnp.int32)) % x_count
    rows_att = rows_att[order]
    rows_att = jnp.transpose(rows_att, (1, 2, 0, 3)).reshape(
        z_count * tok_local, x_count * width_local
    )
    partial = jnp.dot(rows_att, row_proj, preferred_element_type=jnp.float32)
    partial = partial.astype(jnp.bfloat16).reshape(z_count, tok_local, model_width)
    partial = lax.all_to_all(partial, "z", 0, 0, tiled=True)
    projected = jnp.sum(partial.astype(jnp.float32), axis=0)
    hidden = residual.astype(jnp.float32) + projected
    attended = hidden.astype(jnp.bfloat16)
    mean_square = jnp.mean(hidden * hidden, axis=-1, keepdims=True)
    normed = (hidden * lax.rsqrt(mean_square + 1e-05) * norm_gain).astype(jnp.bfloat16)
    devices = req_count * z_count * x_count
    half_units = FF // 2
    pieces = expert_in.shape[2] // half_units
    capacity = max(2, tok_local * TOP * 5 // (EXPERTS * 4))
    lanes = 128
    folds = model_width // lanes
    flat_routes = routes.reshape(-1)
    onehot = (flat_routes[:, None] == jnp.arange(EXPERTS, dtype=jnp.int32)[None, :]).astype(
        jnp.int32
    )
    slot_index = jnp.sum(jnp.cumsum(onehot, axis=0) * onehot, axis=1) - 1
    positions = flat_routes * capacity + slot_index
    token_of = jnp.arange(tok_local * TOP, dtype=jnp.int32) // TOP
    rows_table = jnp.full((EXPERTS * capacity,), tok_local, jnp.int32).at[positions].set(token_of)
    normed_fold = jnp.concatenate(
        [normed.reshape(tok_local, folds, lanes), jnp.zeros((1, folds, lanes), jnp.bfloat16)], axis=0
    )
    slot_rows = normed_fold[rows_table].reshape(EXPERTS, 1, capacity * folds, lanes)
    outgoing = jnp.broadcast_to(slot_rows, (EXPERTS, 2, capacity * folds, lanes))
    outgoing = outgoing.reshape(devices, pieces * capacity * folds, lanes)
    arrived = lax.all_to_all(outgoing, ("req", "z", "x"), 0, 0, tiled=True)
    sources = arrived.shape[0]
    rows = arrived.reshape(sources * capacity, folds, lanes)
    w_in = expert_in[:, :, 0:half_units].reshape(2, folds, lanes, half_units)
    gate_part = jnp.einsum("tkd,kdf->tf", rows, w_in[0], preferred_element_type=jnp.float32)
    up_part = jnp.einsum("tkd,kdf->tf", rows, w_in[1], preferred_element_type=jnp.float32)
    inner = (jax.nn.silu(gate_part) * up_part).astype(jnp.bfloat16)
    half_out = jnp.dot(inner, expert_down, preferred_element_type=jnp.float32).astype(jnp.bfloat16)
    back = half_out.reshape(sources, capacity * folds, lanes)
    returned = lax.all_to_all(back, ("req", "z", "x"), 0, 0, tiled=True)
    halves = returned.reshape(EXPERTS, 2, capacity, folds, lanes)
    summed = (halves[:, 0].astype(jnp.float32) + halves[:, 1].astype(jnp.float32)).reshape(
        EXPERTS * capacity, folds * lanes
    )
    slot_ids = jnp.arange(EXPERTS * capacity, dtype=jnp.int32)
    route_slots = positions.reshape(tok_local, TOP)
    mixing = jnp.sum(
        jnp.where(route_slots[:, :, None] == slot_ids[None, None, :], gate_weights[:, :, None], 0.0),
        axis=1,
    )
    expert_out = jnp.dot(
        mixing, summed, precision=lax.Precision.HIGHEST, preferred_element_type=jnp.float32
    ).astype(jnp.bfloat16)
    return (attended, expert_out)


def solution(mesh):
    req_size, exp_size = mesh.devices.shape
    x_size = 4 if exp_size % 4 == 0 else 1
    sub_mesh = Mesh(
        mesh.devices.reshape(req_size, exp_size // x_size, x_size), ("req", "z", "x")
    )
    exp = ("z", "x")
    flat = ("req", "z", "x")
    return jax.shard_map(
        layer,
        mesh=sub_mesh,
        in_specs=(
            P("req", None, exp),
            P("req", None, None, exp),
            P("req", None, None, exp),
            P("req"),
            P(exp, None),
            P(flat, None),
            P(),
            P(flat, None),
            P(flat, None),
            P(None, None, flat),
            P(flat, None),
        ),
        out_specs=(P(flat, None), P(flat, None)),
        check_vma=False,
    )
```

```python
import jax
import jax.numpy as jnp
from jax import lax
from jax.experimental import pallas as pl
from jax.experimental.pallas import tpu as pltpu
from jax.sharding import Mesh, PartitionSpec as P


HD = 128
EXPERTS = 64
FF = 1024
TOP = 8
TQ = 256


def _attn_kernel(len_ref, q_ref, ck_ref, cv_ref, nk_ref, nv_ref, o_ref):
    r = pl.program_id(0)
    qb = pl.program_id(1)
    length = len_ref[r]
    q = q_ref[0]
    scale = HD ** (-0.5)
    dims = (((1,), (1,)), ((), ()))
    cache_s = lax.dot_general(q, ck_ref[0, 0], dims, preferred_element_type=jnp.float32) * scale
    new_s = lax.dot_general(q, nk_ref[0, 0], dims, preferred_element_type=jnp.float32) * scale
    cache_j = lax.broadcasted_iota(jnp.int32, cache_s.shape, 1)
    cache_s = jnp.where(cache_j < length, cache_s, -1e30)
    row = lax.broadcasted_iota(jnp.int32, new_s.shape, 0) + qb * TQ
    col = lax.broadcasted_iota(jnp.int32, new_s.shape, 1)
    new_s = jnp.where(col <= row, new_s, -1e30)
    peak = jnp.maximum(
        jnp.max(cache_s, axis=1, keepdims=True), jnp.max(new_s, axis=1, keepdims=True)
    )
    cache_w = jnp.exp(cache_s - peak)
    new_w = jnp.exp(new_s - peak)
    denom = jnp.sum(cache_w, axis=1, keepdims=True) + jnp.sum(new_w, axis=1, keepdims=True)
    mixed = jnp.dot(
        cache_w.astype(jnp.bfloat16), cv_ref[0, 0], preferred_element_type=jnp.float32
    ) + jnp.dot(new_w.astype(jnp.bfloat16), nv_ref[0, 0], preferred_element_type=jnp.float32)
    o_ref[0] = (mixed / denom).astype(o_ref.dtype)


def attention_kernel(queries, new_entries, cache_entries, cache_lengths, interpret=False):
    reqs, new_len, width = queries.shape
    cache_len = cache_entries.shape[2]
    grid_spec = pltpu.PrefetchScalarGridSpec(
        num_scalar_prefetch=1,
        grid=(reqs, new_len // TQ),
        in_specs=[
            pl.BlockSpec((1, TQ, width), lambda r, b, lens: (r, b, 0)),
            pl.BlockSpec((1, 1, cache_len, width), lambda r, b, lens: (r, 0, 0, 0)),
            pl.BlockSpec((1, 1, cache_len, width), lambda r, b, lens: (r, 1, 0, 0)),
            pl.BlockSpec((1, 1, new_len, width), lambda r, b, lens: (r, 0, 0, 0)),
            pl.BlockSpec((1, 1, new_len, width), lambda r, b, lens: (r, 1, 0, 0)),
        ],
        out_specs=pl.BlockSpec((1, TQ, width), lambda r, b, lens: (r, b, 0)),
    )
    return pl.pallas_call(
        _attn_kernel,
        grid_spec=grid_spec,
        out_shape=jax.ShapeDtypeStruct((reqs, new_len, width), jnp.bfloat16),
        interpret=interpret,
    )(cache_lengths, queries, cache_entries, cache_entries, new_entries, new_entries)


def layer(
    queries,
    new_entries,
    cache_entries,
    cache_lengths,
    out_proj,
    residual,
    norm_gain,
    routes,
    gate_weights,
    expert_in,
    expert_down,
):
    req_local, new_len, width_local = queries.shape
    tok_local = residual.shape[0]
    model_width = residual.shape[1]

    attention = attention_kernel(queries, new_entries, cache_entries, cache_lengths)
    attention = attention.reshape(req_local * new_len, width_local)
    req_count = lax.axis_size("req")
    z_count = lax.axis_size("z")
    x_count = lax.axis_size("x")
    x_here = lax.axis_index("x")
    shifted = [out_proj]
    for step in range(1, x_count):
        pairs = [(i, (i + step) % x_count) for i in range(x_count)]
        shifted.append(lax.ppermute(out_proj, "x", pairs))
    row_proj = jnp.stack(shifted)
    row_proj = row_proj.reshape(x_count * width_local, model_width)
    rows_att = attention.reshape(z_count, x_count, tok_local, width_local)
    rows_att = jnp.transpose(rows_att, (1, 0, 2, 3))
    rows_att = lax.all_to_all(rows_att, "x", 0, 0, tiled=True)
    order = (x_here - jnp.arange(x_count, dtype=jnp.int32)) % x_count
    rows_att = rows_att[order]
    rows_att = jnp.transpose(rows_att, (1, 2, 0, 3)).reshape(
        z_count * tok_local, x_count * width_local
    )
    partial = jnp.dot(rows_att, row_proj, preferred_element_type=jnp.float32)
    partial = partial.astype(jnp.bfloat16).reshape(z_count, tok_local, model_width)
    partial = lax.all_to_all(partial, "z", 0, 0, tiled=True)
    projected = jnp.sum(partial.astype(jnp.float32), axis=0)
    hidden = residual.astype(jnp.float32) + projected
    attended = hidden.astype(jnp.bfloat16)
    mean_square = jnp.mean(hidden * hidden, axis=-1, keepdims=True)
    normed = (hidden * lax.rsqrt(mean_square + 1e-05) * norm_gain).astype(jnp.bfloat16)
    devices = req_count * z_count * x_count
    half_units = FF // 2
    pieces = expert_in.shape[2] // half_units
    capacity = max(2, tok_local * TOP * 5 // (EXPERTS * 4))
    lanes = 128
    folds = model_width // lanes
    flat_routes = routes.reshape(-1)
    onehot = (flat_routes[:, None] == jnp.arange(EXPERTS, dtype=jnp.int32)[None, :]).astype(
        jnp.int32
    )
    slot_index = jnp.sum(jnp.cumsum(onehot, axis=0) * onehot, axis=1) - 1
    positions = flat_routes * capacity + slot_index
    token_of = jnp.arange(tok_local * TOP, dtype=jnp.int32) // TOP
    rows_table = jnp.full((EXPERTS * capacity,), tok_local, jnp.int32).at[positions].set(token_of)
    normed_fold = jnp.concatenate(
        [normed.reshape(tok_local, folds, lanes), jnp.zeros((1, folds, lanes), jnp.bfloat16)], axis=0
    )
    slot_rows = normed_fold[rows_table].reshape(EXPERTS, 1, capacity * folds, lanes)
    outgoing = jnp.broadcast_to(slot_rows, (EXPERTS, 2, capacity * folds, lanes))
    outgoing = outgoing.reshape(devices, pieces * capacity * folds, lanes)
    arrived = lax.all_to_all(outgoing, ("req", "z", "x"), 0, 0, tiled=True)
    sources = arrived.shape[0]
    rows = arrived.reshape(sources * capacity, folds, lanes)
    w_in = expert_in[:, :, 0:half_units].reshape(2, folds, lanes, half_units)
    gate_part = jnp.einsum("tkd,kdf->tf", rows, w_in[0], preferred_element_type=jnp.float32)
    up_part = jnp.einsum("tkd,kdf->tf", rows, w_in[1], preferred_element_type=jnp.float32)
    inner = (jax.nn.silu(gate_part) * up_part).astype(jnp.bfloat16)
    half_out = jnp.dot(inner, expert_down, preferred_element_type=jnp.float32).astype(jnp.bfloat16)
    back = half_out.reshape(sources, capacity * folds, lanes)
    returned = lax.all_to_all(back, ("req", "z", "x"), 0, 0, tiled=True)
    halves = returned.reshape(EXPERTS, 2, capacity, folds, lanes)
    summed = (halves[:, 0].astype(jnp.float32) + halves[:, 1].astype(jnp.float32)).reshape(
        EXPERTS * capacity, folds * lanes
    )
    slot_ids = jnp.arange(EXPERTS * capacity, dtype=jnp.int32)
    route_slots = positions.reshape(tok_local, TOP)
    mixing = jnp.sum(
        jnp.where(route_slots[:, :, None] == slot_ids[None, None, :], gate_weights[:, :, None], 0.0),
        axis=1,
    )
    expert_out = jnp.dot(
        mixing, summed, precision=lax.Precision.HIGHEST, preferred_element_type=jnp.float32
    ).astype(jnp.bfloat16)
    return (attended, expert_out)


def solution(mesh):
    req_size, exp_size = mesh.devices.shape
    x_size = 4 if exp_size % 4 == 0 else 1
    sub_mesh = Mesh(
        mesh.devices.reshape(req_size, exp_size // x_size, x_size), ("req", "z", "x")
    )
    exp = ("z", "x")
    flat = ("req", "z", "x")
    return jax.shard_map(
        layer,
        mesh=sub_mesh,
        in_specs=(
            P("req", None, exp),
            P("req", None, None, exp),
            P("req", None, None, exp),
            P("req"),
            P(exp, None),
            P(flat, None),
            P(),
            P(flat, None),
            P(flat, None),
            P(None, None, flat),
            P(flat, None),
        ),
        out_specs=(P(flat, None), P(flat, None)),
        check_vma=False,
    )
```

```python
import jax
import jax.numpy as jnp
from jax import lax
from jax.experimental import pallas as pl
from jax.experimental.pallas import tpu as pltpu
from jax.sharding import Mesh, PartitionSpec as P


HD = 128
EXPERTS = 64
FF = 1024
TOP = 8
TQ = 256


def _attn_kernel(len_ref, q_ref, ck_ref, cv_ref, nk_ref, nv_ref, o_ref):
    r = pl.program_id(0)
    qb = pl.program_id(1)
    length = len_ref[r]
    q = q_ref[0]
    scale = HD ** (-0.5)
    dims = (((1,), (1,)), ((), ()))
    cache_s = lax.dot_general(q, ck_ref[0, 0], dims, preferred_element_type=jnp.float32) * scale
    new_s = lax.dot_general(q, nk_ref[0, 0], dims, preferred_element_type=jnp.float32) * scale
    cache_j = lax.broadcasted_iota(jnp.int32, cache_s.shape, 1)
    cache_s = jnp.where(cache_j < length, cache_s, -1e30)
    row = lax.broadcasted_iota(jnp.int32, new_s.shape, 0) + qb * TQ
    col = lax.broadcasted_iota(jnp.int32, new_s.shape, 1)
    new_s = jnp.where(col <= row, new_s, -1e30)
    peak = jnp.maximum(
        jnp.max(cache_s, axis=1, keepdims=True), jnp.max(new_s, axis=1, keepdims=True)
    )
    cache_w = jnp.exp(cache_s - peak)
    new_w = jnp.exp(new_s - peak)
    denom = jnp.sum(cache_w, axis=1, keepdims=True) + jnp.sum(new_w, axis=1, keepdims=True)
    mixed = jnp.dot(
        cache_w.astype(jnp.bfloat16), cv_ref[0, 0], preferred_element_type=jnp.float32
    ) + jnp.dot(new_w.astype(jnp.bfloat16), nv_ref[0, 0], preferred_element_type=jnp.float32)
    o_ref[0] = (mixed / denom).astype(o_ref.dtype)


def attention_kernel(queries, new_entries, cache_entries, cache_lengths, interpret=False):
    reqs, new_len, width = queries.shape
    cache_len = cache_entries.shape[2]
    grid_spec = pltpu.PrefetchScalarGridSpec(
        num_scalar_prefetch=1,
        grid=(reqs, new_len // TQ),
        in_specs=[
            pl.BlockSpec((1, TQ, width), lambda r, b, lens: (r, b, 0)),
            pl.BlockSpec((1, 1, cache_len, width), lambda r, b, lens: (r, 0, 0, 0)),
            pl.BlockSpec((1, 1, cache_len, width), lambda r, b, lens: (r, 1, 0, 0)),
            pl.BlockSpec((1, 1, new_len, width), lambda r, b, lens: (r, 0, 0, 0)),
            pl.BlockSpec((1, 1, new_len, width), lambda r, b, lens: (r, 1, 0, 0)),
        ],
        out_specs=pl.BlockSpec((1, TQ, width), lambda r, b, lens: (r, b, 0)),
    )
    return pl.pallas_call(
        _attn_kernel,
        grid_spec=grid_spec,
        out_shape=jax.ShapeDtypeStruct((reqs, new_len, width), jnp.bfloat16),
        interpret=interpret,
    )(cache_lengths, queries, cache_entries, cache_entries, new_entries, new_entries)


def layer(
    queries,
    new_entries,
    cache_entries,
    cache_lengths,
    out_proj,
    residual,
    norm_gain,
    routes,
    gate_weights,
    expert_in,
    expert_down,
):
    req_local, new_len, width_local = queries.shape
    tok_local = residual.shape[0]
    model_width = residual.shape[1]

    attention = attention_kernel(queries, new_entries, cache_entries, cache_lengths)
    attention = attention.reshape(req_local * new_len, width_local)
    req_count = lax.axis_size("req")
    z_count = lax.axis_size("z")
    x_count = lax.axis_size("x")
    x_here = lax.axis_index("x")
    shifted = [out_proj]
    for step in range(1, x_count):
        pairs = [(i, (i + step) % x_count) for i in range(x_count)]
        shifted.append(lax.ppermute(out_proj, "x", pairs))
    row_proj = jnp.stack(shifted)
    row_proj = row_proj.reshape(x_count * width_local, model_width)
    rows_att = attention.reshape(z_count, x_count, tok_local, width_local)
    rows_att = jnp.transpose(rows_att, (1, 0, 2, 3))
    rows_att = lax.all_to_all(rows_att, "x", 0, 0, tiled=True)
    order = (x_here - jnp.arange(x_count, dtype=jnp.int32)) % x_count
    rows_att = rows_att[order]
    rows_att = jnp.transpose(rows_att, (1, 2, 0, 3)).reshape(
        z_count * tok_local, x_count * width_local
    )
    partial = jnp.dot(rows_att, row_proj, preferred_element_type=jnp.float32)
    partial = partial.astype(jnp.bfloat16).reshape(z_count, tok_local, model_width)
    partial = lax.all_to_all(partial, "z", 0, 0, tiled=True)
    projected = jnp.sum(partial.astype(jnp.float32), axis=0)
    hidden = residual.astype(jnp.float32) + projected
    attended = hidden.astype(jnp.bfloat16)
    mean_square = jnp.mean(hidden * hidden, axis=-1, keepdims=True)
    normed = (hidden * lax.rsqrt(mean_square + 1e-05) * norm_gain).astype(jnp.bfloat16)
    devices = req_count * z_count * x_count
    half_units = FF // 2
    pieces = expert_in.shape[2] // half_units
    capacity = max(2, tok_local * TOP * 5 // (EXPERTS * 4))
    lanes = 128
    folds = model_width // lanes
    flat_routes = routes.reshape(-1)
    onehot = (flat_routes[:, None] == jnp.arange(EXPERTS, dtype=jnp.int32)[None, :]).astype(
        jnp.int32
    )
    slot_index = jnp.sum(jnp.cumsum(onehot, axis=0) * onehot, axis=1) - 1
    positions = flat_routes * capacity + slot_index
    token_of = jnp.arange(tok_local * TOP, dtype=jnp.int32) // TOP
    rows_table = jnp.full((EXPERTS * capacity,), tok_local, jnp.int32).at[positions].set(token_of)
    normed_fold = jnp.concatenate(
        [normed.reshape(tok_local, folds, lanes), jnp.zeros((1, folds, lanes), jnp.bfloat16)], axis=0
    )
    dest_table = jnp.broadcast_to(rows_table.reshape(EXPERTS, 1, capacity), (EXPERTS, 2, capacity))
    outgoing = normed_fold[dest_table.reshape(-1)]
    outgoing = outgoing.reshape(devices, pieces * capacity * folds, lanes)
    arrived = lax.all_to_all(outgoing, ("req", "z", "x"), 0, 0, tiled=True)
    sources = arrived.shape[0]
    rows = arrived.reshape(sources * capacity, folds, lanes)
    w_in = expert_in[:, :, 0:half_units].reshape(2, folds, lanes, half_units)
    gate_part = jnp.einsum("tkd,kdf->tf", rows, w_in[0], preferred_element_type=jnp.float32)
    up_part = jnp.einsum("tkd,kdf->tf", rows, w_in[1], preferred_element_type=jnp.float32)
    inner = (jax.nn.silu(gate_part) * up_part).astype(jnp.bfloat16)
    half_out = jnp.dot(inner, expert_down, preferred_element_type=jnp.float32).astype(jnp.bfloat16)
    back = half_out.reshape(sources, capacity * folds, lanes)
    returned = lax.all_to_all(back, ("req", "z", "x"), 0, 0, tiled=True)
    slot_ids = jnp.arange(EXPERTS * capacity, dtype=jnp.int32)
    route_slots = positions.reshape(tok_local, TOP)
    mixing = jnp.sum(
        jnp.where(route_slots[:, :, None] == slot_ids[None, None, :], gate_weights[:, :, None], 0.0),
        axis=1,
    )
    mixing = jnp.broadcast_to(mixing.reshape(tok_local, EXPERTS, 1, capacity), (tok_local, EXPERTS, 2, capacity))
    mixing = mixing.reshape(tok_local, EXPERTS * 2 * capacity)
    both = returned.reshape(EXPERTS * 2 * capacity, folds, lanes).astype(jnp.float32)
    expert_out = jnp.einsum(
        "ts,skd->tkd", mixing, both, precision=lax.Precision.HIGHEST,
        preferred_element_type=jnp.float32,
    )
    expert_out = expert_out.astype(jnp.bfloat16).reshape(tok_local, model_width)
    return (attended, expert_out)


def solution(mesh):
    req_size, exp_size = mesh.devices.shape
    x_size = 4 if exp_size % 4 == 0 else 1
    sub_mesh = Mesh(
        mesh.devices.reshape(req_size, exp_size // x_size, x_size), ("req", "z", "x")
    )
    exp = ("z", "x")
    flat = ("req", "z", "x")
    return jax.shard_map(
        layer,
        mesh=sub_mesh,
        in_specs=(
            P("req", None, exp),
            P("req", None, None, exp),
            P("req", None, None, exp),
            P("req"),
            P(exp, None),
            P(flat, None),
            P(),
            P(flat, None),
            P(flat, None),
            P(None, None, flat),
            P(flat, None),
        ),
        out_specs=(P(flat, None), P(flat, None)),
        check_vma=False,
    )
```

```python
import numpy as np
import jax
import jax.numpy as jnp
from jax import lax
from jax.experimental import pallas as pl
from jax.experimental.pallas import tpu as pltpu
from jax.sharding import Mesh, PartitionSpec as P


HD = 128
EXPERTS = 64
FF = 1024
TOP = 8
TQ = 256


def _attn_kernel(len_ref, q_ref, ck_ref, cv_ref, nk_ref, nv_ref, o_ref):
    r = pl.program_id(0)
    qb = pl.program_id(1)
    length = len_ref[r]
    q = q_ref[0]
    scale = HD ** (-0.5)
    dims = (((1,), (1,)), ((), ()))
    cache_s = lax.dot_general(q, ck_ref[0, 0], dims, preferred_element_type=jnp.float32) * scale
    new_s = lax.dot_general(q, nk_ref[0, 0], dims, preferred_element_type=jnp.float32) * scale
    cache_j = lax.broadcasted_iota(jnp.int32, cache_s.shape, 1)
    cache_s = jnp.where(cache_j < length, cache_s, -1e30)
    row = lax.broadcasted_iota(jnp.int32, new_s.shape, 0) + qb * TQ
    col = lax.broadcasted_iota(jnp.int32, new_s.shape, 1)
    new_s = jnp.where(col <= row, new_s, -1e30)
    peak = jnp.maximum(
        jnp.max(cache_s, axis=1, keepdims=True), jnp.max(new_s, axis=1, keepdims=True)
    )
    cache_w = jnp.exp(cache_s - peak)
    new_w = jnp.exp(new_s - peak)
    denom = jnp.sum(cache_w, axis=1, keepdims=True) + jnp.sum(new_w, axis=1, keepdims=True)
    mixed = jnp.dot(
        cache_w.astype(jnp.bfloat16), cv_ref[0, 0], preferred_element_type=jnp.float32
    ) + jnp.dot(new_w.astype(jnp.bfloat16), nv_ref[0, 0], preferred_element_type=jnp.float32)
    o_ref[0] = (mixed / denom).astype(o_ref.dtype)


def attention_kernel(queries, new_entries, cache_entries, cache_lengths, interpret=False):
    reqs, new_len, width = queries.shape
    cache_len = cache_entries.shape[2]
    grid_spec = pltpu.PrefetchScalarGridSpec(
        num_scalar_prefetch=1,
        grid=(reqs, new_len // TQ),
        in_specs=[
            pl.BlockSpec((1, TQ, width), lambda r, b, lens: (r, b, 0)),
            pl.BlockSpec((1, 1, cache_len, width), lambda r, b, lens: (r, 0, 0, 0)),
            pl.BlockSpec((1, 1, cache_len, width), lambda r, b, lens: (r, 1, 0, 0)),
            pl.BlockSpec((1, 1, new_len, width), lambda r, b, lens: (r, 0, 0, 0)),
            pl.BlockSpec((1, 1, new_len, width), lambda r, b, lens: (r, 1, 0, 0)),
        ],
        out_specs=pl.BlockSpec((1, TQ, width), lambda r, b, lens: (r, b, 0)),
    )
    return pl.pallas_call(
        _attn_kernel,
        grid_spec=grid_spec,
        out_shape=jax.ShapeDtypeStruct((reqs, new_len, width), jnp.bfloat16),
        interpret=interpret,
    )(cache_lengths, queries, cache_entries, cache_entries, new_entries, new_entries)


def layer(
    queries,
    new_entries,
    cache_entries,
    cache_lengths,
    out_proj,
    residual,
    norm_gain,
    routes,
    gate_weights,
    expert_in,
    expert_down,
):
    req_local, new_len, width_local = queries.shape
    tok_local = residual.shape[0]
    model_width = residual.shape[1]

    attention = attention_kernel(queries, new_entries, cache_entries, cache_lengths)
    attention = attention.reshape(req_local * new_len, width_local)
    y_count = lax.axis_size("y")
    c_count = lax.axis_size("c")
    req_count = y_count * c_count
    z_count = lax.axis_size("z")
    x_count = lax.axis_size("x")
    swap_pairs = []
    for c in range(c_count):
        for x in range(x_count):
            partner = (1 - c, x + 1 - 2 * (x % 2)) if c != x % 2 else (c, x)
            swap_pairs.append((c * x_count + x, partner[0] * x_count + partner[1]))
    my_in = lax.ppermute(expert_in, ("c", "x"), swap_pairs)
    my_down = lax.ppermute(expert_down, ("c", "x"), swap_pairs)
    x_here = lax.axis_index("x")
    shifted = [out_proj]
    for step in range(1, x_count):
        pairs = [(i, (i + step) % x_count) for i in range(x_count)]
        shifted.append(lax.ppermute(out_proj, "x", pairs))
    row_proj = jnp.stack(shifted)
    row_proj = row_proj.reshape(x_count * width_local, model_width)
    rows_att = attention.reshape(z_count, x_count, tok_local, width_local)
    rows_att = jnp.transpose(rows_att, (1, 0, 2, 3))
    rows_att = lax.all_to_all(rows_att, "x", 0, 0, tiled=True)
    order = (x_here - jnp.arange(x_count, dtype=jnp.int32)) % x_count
    rows_att = rows_att[order]
    rows_att = jnp.transpose(rows_att, (1, 2, 0, 3)).reshape(
        z_count * tok_local, x_count * width_local
    )
    partial = jnp.dot(rows_att, row_proj, preferred_element_type=jnp.float32)
    partial = partial.astype(jnp.bfloat16).reshape(z_count, tok_local, model_width)
    partial = lax.all_to_all(partial, "z", 0, 0, tiled=True)
    projected = jnp.sum(partial.astype(jnp.float32), axis=0)
    hidden = residual.astype(jnp.float32) + projected
    attended = hidden.astype(jnp.bfloat16)
    mean_square = jnp.mean(hidden * hidden, axis=-1, keepdims=True)
    normed = (hidden * lax.rsqrt(mean_square + 1e-05) * norm_gain).astype(jnp.bfloat16)
    devices = req_count * z_count * x_count
    half_units = FF // 2
    capacity = max(2, tok_local * TOP * 5 // (EXPERTS * 4))
    lanes = 128
    folds = model_width // lanes
    flat_routes = routes.reshape(-1)
    onehot = (flat_routes[:, None] == jnp.arange(EXPERTS, dtype=jnp.int32)[None, :]).astype(
        jnp.int32
    )
    slot_index = jnp.sum(jnp.cumsum(onehot, axis=0) * onehot, axis=1) - 1
    positions = flat_routes * capacity + slot_index
    token_of = jnp.arange(tok_local * TOP, dtype=jnp.int32) // TOP
    rows_table = jnp.full((EXPERTS * capacity,), tok_local, jnp.int32).at[positions].set(token_of)
    normed_fold = jnp.concatenate(
        [normed.reshape(tok_local, folds, lanes), jnp.zeros((1, folds, lanes), jnp.bfloat16)], axis=0
    )
    split = capacity // c_count
    dev = np.arange(devices)
    dev_c = (dev // (z_count * x_count)) % c_count
    dev_y = dev // (c_count * z_count * x_count)
    dev_zx = dev % (z_count * x_count)
    dev_x = dev % x_count
    chip_expert = ((dev_y * c_count + dev_x % c_count) * z_count * x_count + dev_zx) // 2
    slot_of = (
        chip_expert[:, None] * capacity + dev_c[:, None] * split + np.arange(split)[None, :]
    ).reshape(-1)
    slot_of = jnp.asarray(slot_of, jnp.int32)
    outgoing = normed_fold[rows_table[slot_of]]
    outgoing = outgoing.reshape(devices, split * folds, lanes)
    arrived = lax.all_to_all(outgoing, ("y", "c", "z", "x"), 0, 0, tiled=True)
    other = lax.ppermute(arrived, "c", [(0, 1), (1, 0)])
    sources = arrived.shape[0]
    rows = jnp.concatenate([arrived, other], axis=0).reshape(2 * sources * split, folds, lanes)
    w_in = my_in.reshape(2, folds, lanes, half_units)
    gate_part = jnp.einsum("tkd,kdf->tf", rows, w_in[0], preferred_element_type=jnp.float32)
    up_part = jnp.einsum("tkd,kdf->tf", rows, w_in[1], preferred_element_type=jnp.float32)
    inner = (jax.nn.silu(gate_part) * up_part).astype(jnp.bfloat16)
    half_out = jnp.dot(inner, my_down, preferred_element_type=jnp.float32).astype(jnp.bfloat16)
    half_out = half_out.reshape(2, sources, split * folds, lanes)
    theirs = lax.ppermute(half_out[1], "c", [(0, 1), (1, 0)])
    both = (half_out[0].astype(jnp.float32) + theirs.astype(jnp.float32)).astype(jnp.bfloat16)
    returned = lax.all_to_all(both, ("y", "c", "z", "x"), 0, 0, tiled=True)
    slot_ids = jnp.arange(EXPERTS * capacity, dtype=jnp.int32)
    route_slots = positions.reshape(tok_local, TOP)
    mixing = jnp.sum(
        jnp.where(route_slots[:, :, None] == slot_ids[None, None, :], gate_weights[:, :, None], 0.0),
        axis=1,
    )
    mixing = mixing[:, slot_of]
    summed = returned.reshape(devices * split, folds, lanes).astype(jnp.float32)
    expert_out = jnp.einsum(
        "ts,skd->tkd", mixing, summed, precision=lax.Precision.HIGHEST,
        preferred_element_type=jnp.float32,
    )
    expert_out = expert_out.astype(jnp.bfloat16).reshape(tok_local, model_width)
    return (attended, expert_out)


def solution(mesh):
    req_size, exp_size = mesh.devices.shape
    x_size = 4 if exp_size % 4 == 0 else 1
    sub_mesh = Mesh(
        mesh.devices.reshape(req_size // 2, 2, exp_size // x_size, x_size), ("y", "c", "z", "x")
    )
    exp = ("z", "x")
    req = ("y", "c")
    flat = ("y", "c", "z", "x")
    return jax.shard_map(
        layer,
        mesh=sub_mesh,
        in_specs=(
            P(req, None, exp),
            P(req, None, None, exp),
            P(req, None, None, exp),
            P(req),
            P(exp, None),
            P(flat, None),
            P(),
            P(flat, None),
            P(flat, None),
            P(None, None, flat),
            P(flat, None),
        ),
        out_specs=(P(flat, None), P(flat, None)),
        check_vma=False,
    )
```

```python
import jax
import jax.numpy as jnp
from jax import lax
from jax.experimental import pallas as pl
from jax.experimental.pallas import tpu as pltpu
from jax.sharding import Mesh, PartitionSpec as P


HD = 128
EXPERTS = 64
FF = 1024
TOP = 8
TQ = 256


def _attn_kernel(len_ref, q_ref, ck_ref, cv_ref, nk_ref, nv_ref, o_ref):
    r = pl.program_id(0)
    qb = pl.program_id(1)
    length = len_ref[r]
    q = q_ref[0]
    scale = HD ** (-0.5)
    dims = (((1,), (1,)), ((), ()))
    cache_s = lax.dot_general(q, ck_ref[0, 0], dims, preferred_element_type=jnp.float32) * scale
    new_s = lax.dot_general(q, nk_ref[0, 0], dims, preferred_element_type=jnp.float32) * scale
    cache_j = lax.broadcasted_iota(jnp.int32, cache_s.shape, 1)
    cache_s = jnp.where(cache_j < length, cache_s, -1e30)
    row = lax.broadcasted_iota(jnp.int32, new_s.shape, 0) + qb * TQ
    col = lax.broadcasted_iota(jnp.int32, new_s.shape, 1)
    new_s = jnp.where(col <= row, new_s, -1e30)
    peak = jnp.maximum(
        jnp.max(cache_s, axis=1, keepdims=True), jnp.max(new_s, axis=1, keepdims=True)
    )
    cache_w = jnp.exp(cache_s - peak)
    new_w = jnp.exp(new_s - peak)
    denom = jnp.sum(cache_w, axis=1, keepdims=True) + jnp.sum(new_w, axis=1, keepdims=True)
    mixed = jnp.dot(
        cache_w.astype(jnp.bfloat16), cv_ref[0, 0], preferred_element_type=jnp.float32
    ) + jnp.dot(new_w.astype(jnp.bfloat16), nv_ref[0, 0], preferred_element_type=jnp.float32)
    o_ref[0] = (mixed / denom).astype(o_ref.dtype)


def attention_kernel(queries, new_entries, cache_entries, cache_lengths, interpret=False):
    reqs, new_len, width = queries.shape
    cache_len = cache_entries.shape[2]
    grid_spec = pltpu.PrefetchScalarGridSpec(
        num_scalar_prefetch=1,
        grid=(reqs, new_len // TQ),
        in_specs=[
            pl.BlockSpec((1, TQ, width), lambda r, b, lens: (r, b, 0)),
            pl.BlockSpec((1, 1, cache_len, width), lambda r, b, lens: (r, 0, 0, 0)),
            pl.BlockSpec((1, 1, cache_len, width), lambda r, b, lens: (r, 1, 0, 0)),
            pl.BlockSpec((1, 1, new_len, width), lambda r, b, lens: (r, 0, 0, 0)),
            pl.BlockSpec((1, 1, new_len, width), lambda r, b, lens: (r, 1, 0, 0)),
        ],
        out_specs=pl.BlockSpec((1, TQ, width), lambda r, b, lens: (r, b, 0)),
    )
    return pl.pallas_call(
        _attn_kernel,
        grid_spec=grid_spec,
        out_shape=jax.ShapeDtypeStruct((reqs, new_len, width), jnp.bfloat16),
        interpret=interpret,
    )(cache_lengths, queries, cache_entries, cache_entries, new_entries, new_entries)


def layer(
    queries,
    new_entries,
    cache_entries,
    cache_lengths,
    out_proj,
    residual,
    norm_gain,
    routes,
    gate_weights,
    expert_in,
    expert_down,
):
    req_local, new_len, width_local = queries.shape
    tok_local = residual.shape[0]
    model_width = residual.shape[1]

    attention = attention_kernel(queries, new_entries, cache_entries, cache_lengths)
    attention = attention.reshape(req_local * new_len, width_local)
    req_count = lax.axis_size("req")
    z_count = lax.axis_size("z")
    x_count = lax.axis_size("x")
    x_here = lax.axis_index("x")
    shifted = [out_proj]
    for step in range(1, x_count):
        pairs = [(i, (i + step) % x_count) for i in range(x_count)]
        shifted.append(lax.ppermute(out_proj, "x", pairs))
    row_proj = jnp.stack(shifted)
    row_proj = row_proj.reshape(x_count * width_local, model_width)
    rows_att = attention.reshape(z_count, x_count, tok_local, width_local)
    rows_att = jnp.transpose(rows_att, (1, 0, 2, 3))
    rows_att = lax.all_to_all(rows_att, "x", 0, 0, tiled=True)
    order = (x_here - jnp.arange(x_count, dtype=jnp.int32)) % x_count
    rows_att = rows_att[order]
    rows_att = jnp.transpose(rows_att, (1, 2, 0, 3)).reshape(
        z_count * tok_local, x_count * width_local
    )
    partial = jnp.dot(rows_att, row_proj, preferred_element_type=jnp.float32)
    partial = partial.astype(jnp.bfloat16).reshape(z_count, tok_local, model_width)
    partial = lax.all_to_all(partial, "z", 0, 0, tiled=True)
    projected = jnp.sum(partial.astype(jnp.float32), axis=0)
    hidden = residual.astype(jnp.float32) + projected
    attended = hidden.astype(jnp.bfloat16)
    mean_square = jnp.mean(hidden * hidden, axis=-1, keepdims=True)
    normed = (hidden * lax.rsqrt(mean_square + 1e-05) * norm_gain).astype(jnp.bfloat16)
    devices = req_count * z_count * x_count
    half_units = FF // 2
    pieces = expert_in.shape[2] // half_units
    capacity = max(2, tok_local * TOP * 5 // (EXPERTS * 4))
    lanes = 128
    folds = model_width // lanes
    flat_routes = routes.reshape(-1)
    onehot = (flat_routes[:, None] == jnp.arange(EXPERTS, dtype=jnp.int32)[None, :]).astype(
        jnp.int32
    )
    slot_index = jnp.sum(jnp.cumsum(onehot, axis=0) * onehot, axis=1) - 1
    positions = flat_routes * capacity + slot_index
    token_of = jnp.arange(tok_local * TOP, dtype=jnp.int32) // TOP
    rows_table = jnp.full((EXPERTS * capacity,), tok_local, jnp.int32).at[positions].set(token_of)
    normed_fold = jnp.concatenate(
        [normed.reshape(tok_local, folds, lanes), jnp.zeros((1, folds, lanes), jnp.bfloat16)], axis=0
    )
    dest_table = jnp.broadcast_to(rows_table.reshape(EXPERTS, 1, capacity), (EXPERTS, 2, capacity))
    outgoing = normed_fold[dest_table.reshape(-1)]
    outgoing = outgoing.reshape(devices, pieces * capacity * folds, lanes)
    arrived = lax.all_to_all(outgoing, ("req", "z", "x"), 0, 0, tiled=True)
    sources = arrived.shape[0]
    rows = arrived.reshape(sources * capacity, folds, lanes)
    w_in = jnp.concatenate([expert_in[0, :, 0:half_units], expert_in[1, :, 0:half_units]], axis=1)
    w_in = w_in.reshape(folds, lanes, 2 * half_units)
    both_parts = jnp.einsum("tkd,kdf->tf", rows, w_in, preferred_element_type=jnp.float32)
    gate_part = both_parts[:, :half_units]
    up_part = both_parts[:, half_units:]
    inner = (jax.nn.silu(gate_part) * up_part).astype(jnp.bfloat16)
    half_out = jnp.dot(inner, expert_down, preferred_element_type=jnp.float32).astype(jnp.bfloat16)
    back = half_out.reshape(sources, capacity * folds, lanes)
    returned = lax.all_to_all(back, ("req", "z", "x"), 0, 0, tiled=True)
    slot_ids = jnp.arange(EXPERTS * capacity, dtype=jnp.int32)
    route_slots = positions.reshape(tok_local, TOP)
    mixing = jnp.sum(
        jnp.where(route_slots[:, :, None] == slot_ids[None, None, :], gate_weights[:, :, None], 0.0),
        axis=1,
    )
    mixing = jnp.broadcast_to(mixing.reshape(tok_local, EXPERTS, 1, capacity), (tok_local, EXPERTS, 2, capacity))
    mixing = mixing.reshape(tok_local, EXPERTS * 2 * capacity)
    both = returned.reshape(EXPERTS * 2 * capacity, folds, lanes)
    mixing_hi = mixing.astype(jnp.bfloat16)
    mixing_lo = (mixing - mixing_hi.astype(jnp.float32)).astype(jnp.bfloat16)
    expert_out = jnp.einsum(
        "ts,skd->tkd", mixing_hi, both, preferred_element_type=jnp.float32
    ) + jnp.einsum("ts,skd->tkd", mixing_lo, both, preferred_element_type=jnp.float32)
    expert_out = expert_out.astype(jnp.bfloat16).reshape(tok_local, model_width)
    return (attended, expert_out)


def solution(mesh):
    req_size, exp_size = mesh.devices.shape
    x_size = 4 if exp_size % 4 == 0 else 1
    sub_mesh = Mesh(
        mesh.devices.reshape(req_size, exp_size // x_size, x_size), ("req", "z", "x")
    )
    exp = ("z", "x")
    flat = ("req", "z", "x")
    return jax.shard_map(
        layer,
        mesh=sub_mesh,
        in_specs=(
            P("req", None, exp),
            P("req", None, None, exp),
            P("req", None, None, exp),
            P("req"),
            P(exp, None),
            P(flat, None),
            P(),
            P(flat, None),
            P(flat, None),
            P(None, None, flat),
            P(flat, None),
        ),
        out_specs=(P(flat, None), P(flat, None)),
        check_vma=False,
    )
```

```python
import functools

import jax
import jax.numpy as jnp
from jax import lax
from jax.experimental import pallas as pl
from jax.experimental.pallas import tpu as pltpu
from jax.sharding import Mesh, PartitionSpec as P


HD = 128
EXPERTS = 64
FF = 1024
TOP = 8
TQ = 256


def _attn_kernel(len_ref, q_ref, ck_ref, cv_ref, nk_ref, nv_ref, o_ref, *, r):
    qb = pl.program_id(1)
    length = len_ref[r]
    q = q_ref[0]
    scale = HD ** (-0.5)
    dims = (((1,), (1,)), ((), ()))
    cache_s = lax.dot_general(q, ck_ref[0, 0], dims, preferred_element_type=jnp.float32) * scale
    new_s = lax.dot_general(q, nk_ref[0, 0], dims, preferred_element_type=jnp.float32) * scale
    cache_j = lax.broadcasted_iota(jnp.int32, cache_s.shape, 1)
    cache_s = jnp.where(cache_j < length, cache_s, -1e30)
    row = lax.broadcasted_iota(jnp.int32, new_s.shape, 0) + qb * TQ
    col = lax.broadcasted_iota(jnp.int32, new_s.shape, 1)
    new_s = jnp.where(col <= row, new_s, -1e30)
    peak = jnp.maximum(
        jnp.max(cache_s, axis=1, keepdims=True), jnp.max(new_s, axis=1, keepdims=True)
    )
    cache_w = jnp.exp(cache_s - peak)
    new_w = jnp.exp(new_s - peak)
    denom = jnp.sum(cache_w, axis=1, keepdims=True) + jnp.sum(new_w, axis=1, keepdims=True)
    mixed = jnp.dot(
        cache_w.astype(jnp.bfloat16), cv_ref[0, 0], preferred_element_type=jnp.float32
    ) + jnp.dot(new_w.astype(jnp.bfloat16), nv_ref[0, 0], preferred_element_type=jnp.float32)
    o_ref[0] = (mixed / denom).astype(o_ref.dtype)


def attention_kernel(queries, new_entries, cache_entries, cache_lengths, req, interpret=False):
    _, new_len, width = queries.shape
    cache_len = cache_entries.shape[2]
    grid_spec = pltpu.PrefetchScalarGridSpec(
        num_scalar_prefetch=1,
        grid=(1, new_len // TQ),
        in_specs=[
            pl.BlockSpec((1, TQ, width), lambda r, b, lens: (req, b, 0)),
            pl.BlockSpec((1, 1, cache_len, width), lambda r, b, lens: (req, 0, 0, 0)),
            pl.BlockSpec((1, 1, cache_len, width), lambda r, b, lens: (req, 1, 0, 0)),
            pl.BlockSpec((1, 1, new_len, width), lambda r, b, lens: (req, 0, 0, 0)),
            pl.BlockSpec((1, 1, new_len, width), lambda r, b, lens: (req, 1, 0, 0)),
        ],
        out_specs=pl.BlockSpec((1, TQ, width), lambda r, b, lens: (0, b, 0)),
    )
    return pl.pallas_call(
        functools.partial(_attn_kernel, r=req),
        grid_spec=grid_spec,
        out_shape=jax.ShapeDtypeStruct((1, new_len, width), jnp.bfloat16),
        interpret=interpret,
    )(cache_lengths, queries, cache_entries, cache_entries, new_entries, new_entries)


def layer(
    queries,
    new_entries,
    cache_entries,
    cache_lengths,
    out_proj,
    residual,
    norm_gain,
    routes,
    gate_weights,
    expert_in,
    expert_down,
):
    req_local, _, width_local = queries.shape
    tok_local = residual.shape[0]
    model_width = residual.shape[1]

    req_count = lax.axis_size("req")
    z_count = lax.axis_size("z")
    x_count = lax.axis_size("x")
    x_here = lax.axis_index("x")
    shifted = [out_proj]
    for step in range(1, x_count):
        pairs = [(i, (i + step) % x_count) for i in range(x_count)]
        shifted.append(lax.ppermute(out_proj, "x", pairs))
    row_proj = jnp.stack(shifted)
    row_proj = row_proj.reshape(x_count * width_local, model_width)
    parts = []
    for req in range(req_local):
        att_req = attention_kernel(queries, new_entries, cache_entries, cache_lengths, req)
        att_req = att_req.reshape(z_count // req_local, x_count, tok_local, width_local)
        att_req = jnp.transpose(att_req, (1, 0, 2, 3))
        parts.append(lax.all_to_all(att_req, "x", 0, 0, tiled=True))
    rows_att = jnp.concatenate(parts, axis=1)
    order = (x_here - jnp.arange(x_count, dtype=jnp.int32)) % x_count
    rows_att = rows_att[order]
    rows_att = jnp.transpose(rows_att, (1, 2, 0, 3)).reshape(
        z_count * tok_local, x_count * width_local
    )
    partial = jnp.dot(rows_att, row_proj, preferred_element_type=jnp.float32)
    partial = partial.astype(jnp.bfloat16).reshape(z_count, tok_local, model_width)
    partial = lax.all_to_all(partial, "z", 0, 0, tiled=True)
    projected = jnp.sum(partial.astype(jnp.float32), axis=0)
    hidden = residual.astype(jnp.float32) + projected
    attended = hidden.astype(jnp.bfloat16)
    mean_square = jnp.mean(hidden * hidden, axis=-1, keepdims=True)
    normed = (hidden * lax.rsqrt(mean_square + 1e-05) * norm_gain).astype(jnp.bfloat16)
    devices = req_count * z_count * x_count
    half_units = FF // 2
    pieces = expert_in.shape[2] // half_units
    capacity = max(2, tok_local * TOP * 5 // (EXPERTS * 4))
    lanes = 128
    folds = model_width // lanes
    flat_routes = routes.reshape(-1)
    onehot = (flat_routes[:, None] == jnp.arange(EXPERTS, dtype=jnp.int32)[None, :]).astype(
        jnp.int32
    )
    slot_index = jnp.sum(jnp.cumsum(onehot, axis=0) * onehot, axis=1) - 1
    positions = flat_routes * capacity + slot_index
    token_of = jnp.arange(tok_local * TOP, dtype=jnp.int32) // TOP
    rows_table = jnp.full((EXPERTS * capacity,), tok_local, jnp.int32).at[positions].set(token_of)
    normed_fold = jnp.concatenate(
        [normed.reshape(tok_local, folds, lanes), jnp.zeros((1, folds, lanes), jnp.bfloat16)], axis=0
    )
    dest_table = jnp.broadcast_to(rows_table.reshape(EXPERTS, 1, capacity), (EXPERTS, 2, capacity))
    outgoing = normed_fold[dest_table.reshape(-1)]
    outgoing = outgoing.reshape(devices, pieces * capacity * folds, lanes)
    arrived = lax.all_to_all(outgoing, ("req", "z", "x"), 0, 0, tiled=True)
    sources = arrived.shape[0]
    rows = arrived.reshape(sources * capacity, folds, lanes)
    w_in = jnp.concatenate([expert_in[0, :, 0:half_units], expert_in[1, :, 0:half_units]], axis=1)
    w_in = w_in.reshape(folds, lanes, 2 * half_units)
    both_parts = jnp.einsum("tkd,kdf->tf", rows, w_in, preferred_element_type=jnp.float32)
    gate_part = both_parts[:, :half_units]
    up_part = both_parts[:, half_units:]
    inner = (jax.nn.silu(gate_part) * up_part).astype(jnp.bfloat16)
    half_out = jnp.dot(inner, expert_down, preferred_element_type=jnp.float32).astype(jnp.bfloat16)
    back = half_out.reshape(sources, capacity * folds, lanes)
    returned = lax.all_to_all(back, ("req", "z", "x"), 0, 0, tiled=True)
    slot_ids = jnp.arange(EXPERTS * capacity, dtype=jnp.int32)
    route_slots = positions.reshape(tok_local, TOP)
    mixing = jnp.sum(
        jnp.where(route_slots[:, :, None] == slot_ids[None, None, :], gate_weights[:, :, None], 0.0),
        axis=1,
    )
    mixing = jnp.broadcast_to(mixing.reshape(tok_local, EXPERTS, 1, capacity), (tok_local, EXPERTS, 2, capacity))
    mixing = mixing.reshape(tok_local, EXPERTS * 2 * capacity)
    both = returned.reshape(EXPERTS * 2 * capacity, folds, lanes).astype(jnp.float32)
    expert_out = jnp.einsum(
        "ts,skd->tkd", mixing, both, precision=lax.Precision.HIGHEST,
        preferred_element_type=jnp.float32,
    )
    expert_out = expert_out.astype(jnp.bfloat16).reshape(tok_local, model_width)
    return (attended, expert_out)


def solution(mesh):
    req_size, exp_size = mesh.devices.shape
    x_size = 4 if exp_size % 4 == 0 else 1
    sub_mesh = Mesh(
        mesh.devices.reshape(req_size, exp_size // x_size, x_size), ("req", "z", "x")
    )
    exp = ("z", "x")
    flat = ("req", "z", "x")
    return jax.shard_map(
        layer,
        mesh=sub_mesh,
        in_specs=(
            P("req", None, exp),
            P("req", None, None, exp),
            P("req", None, None, exp),
            P("req"),
            P(exp, None),
            P(flat, None),
            P(),
            P(flat, None),
            P(flat, None),
            P(None, None, flat),
            P(flat, None),
        ),
        out_specs=(P(flat, None), P(flat, None)),
        check_vma=False,
    )
```

```python
import jax
import jax.numpy as jnp
from jax import lax
from jax.experimental import pallas as pl
from jax.experimental.pallas import tpu as pltpu
from jax.sharding import Mesh, PartitionSpec as P


HD = 128
EXPERTS = 64
FF = 1024
TOP = 8
TQ = 128


def _attn_kernel(len_ref, q_ref, ck_ref, cv_ref, nk_ref, nv_ref, o_ref):
    r = pl.program_id(0)
    qb = pl.program_id(1)
    length = len_ref[r]
    q = q_ref[0]
    scale = HD ** (-0.5)
    dims = (((1,), (1,)), ((), ()))
    cache_s = lax.dot_general(q, ck_ref[0, 0], dims, preferred_element_type=jnp.float32) * scale
    new_s = lax.dot_general(q, nk_ref[0, 0], dims, preferred_element_type=jnp.float32) * scale
    cache_j = lax.broadcasted_iota(jnp.int32, cache_s.shape, 1)
    cache_s = jnp.where(cache_j < length, cache_s, -1e30)
    row = lax.broadcasted_iota(jnp.int32, new_s.shape, 0) + qb * TQ
    col = lax.broadcasted_iota(jnp.int32, new_s.shape, 1)
    new_s = jnp.where(col <= row, new_s, -1e30)
    peak = jnp.maximum(
        jnp.max(cache_s, axis=1, keepdims=True), jnp.max(new_s, axis=1, keepdims=True)
    )
    cache_w = jnp.exp(cache_s - peak)
    new_w = jnp.exp(new_s - peak)
    denom = jnp.sum(cache_w, axis=1, keepdims=True) + jnp.sum(new_w, axis=1, keepdims=True)
    mixed = jnp.dot(
        cache_w.astype(jnp.bfloat16), cv_ref[0, 0], preferred_element_type=jnp.float32
    ) + jnp.dot(new_w.astype(jnp.bfloat16), nv_ref[0, 0], preferred_element_type=jnp.float32)
    o_ref[0] = (mixed / denom).astype(o_ref.dtype)


def attention_kernel(queries, new_entries, cache_entries, cache_lengths, interpret=False):
    reqs, new_len, width = queries.shape
    cache_len = cache_entries.shape[2]
    grid_spec = pltpu.PrefetchScalarGridSpec(
        num_scalar_prefetch=1,
        grid=(reqs, new_len // TQ),
        in_specs=[
            pl.BlockSpec((1, TQ, width), lambda r, b, lens: (r, b, 0)),
            pl.BlockSpec((1, 1, cache_len, width), lambda r, b, lens: (r, 0, 0, 0)),
            pl.BlockSpec((1, 1, cache_len, width), lambda r, b, lens: (r, 1, 0, 0)),
            pl.BlockSpec((1, 1, new_len, width), lambda r, b, lens: (r, 0, 0, 0)),
            pl.BlockSpec((1, 1, new_len, width), lambda r, b, lens: (r, 1, 0, 0)),
        ],
        out_specs=pl.BlockSpec((1, TQ, width), lambda r, b, lens: (r, b, 0)),
    )
    return pl.pallas_call(
        _attn_kernel,
        grid_spec=grid_spec,
        out_shape=jax.ShapeDtypeStruct((reqs, new_len, width), jnp.bfloat16),
        interpret=interpret,
    )(cache_lengths, queries, cache_entries, cache_entries, new_entries, new_entries)


def layer(
    queries,
    new_entries,
    cache_entries,
    cache_lengths,
    out_proj,
    residual,
    norm_gain,
    routes,
    gate_weights,
    expert_in,
    expert_down,
):
    req_local, new_len, width_local = queries.shape
    tok_local = residual.shape[0]
    model_width = residual.shape[1]

    attention = attention_kernel(queries, new_entries, cache_entries, cache_lengths)
    attention = attention.reshape(req_local * new_len, width_local)
    req_count = lax.axis_size("req")
    z_count = lax.axis_size("z")
    x_count = lax.axis_size("x")
    x_here = lax.axis_index("x")
    shifted = [out_proj]
    for step in range(1, x_count):
        pairs = [(i, (i + step) % x_count) for i in range(x_count)]
        shifted.append(lax.ppermute(out_proj, "x", pairs))
    row_proj = jnp.stack(shifted)
    row_proj = row_proj.reshape(x_count * width_local, model_width)
    rows_att = attention.reshape(z_count, x_count, tok_local, width_local)
    rows_att = jnp.transpose(rows_att, (1, 0, 2, 3))
    rows_att = lax.all_to_all(rows_att, "x", 0, 0, tiled=True)
    order = (x_here - jnp.arange(x_count, dtype=jnp.int32)) % x_count
    rows_att = rows_att[order]
    rows_att = jnp.transpose(rows_att, (1, 2, 0, 3)).reshape(
        z_count * tok_local, x_count * width_local
    )
    partial = jnp.dot(rows_att, row_proj, preferred_element_type=jnp.float32)
    partial = partial.astype(jnp.bfloat16).reshape(z_count, tok_local, model_width)
    partial = lax.all_to_all(partial, "z", 0, 0, tiled=True)
    projected = jnp.sum(partial.astype(jnp.float32), axis=0)
    hidden = residual.astype(jnp.float32) + projected
    attended = hidden.astype(jnp.bfloat16)
    mean_square = jnp.mean(hidden * hidden, axis=-1, keepdims=True)
    normed = (hidden * lax.rsqrt(mean_square + 1e-05) * norm_gain).astype(jnp.bfloat16)
    devices = req_count * z_count * x_count
    half_units = FF // 2
    pieces = expert_in.shape[2] // half_units
    capacity = max(2, tok_local * TOP * 5 // (EXPERTS * 4))
    lanes = 128
    folds = model_width // lanes
    flat_routes = routes.reshape(-1)
    onehot = (flat_routes[:, None] == jnp.arange(EXPERTS, dtype=jnp.int32)[None, :]).astype(
        jnp.int32
    )
    slot_index = jnp.sum(jnp.cumsum(onehot, axis=0) * onehot, axis=1) - 1
    positions = flat_routes * capacity + slot_index
    token_of = jnp.arange(tok_local * TOP, dtype=jnp.int32) // TOP
    rows_table = jnp.full((EXPERTS * capacity,), tok_local, jnp.int32).at[positions].set(token_of)
    normed_fold = jnp.concatenate(
        [normed.reshape(tok_local, folds, lanes), jnp.zeros((1, folds, lanes), jnp.bfloat16)], axis=0
    )
    dest_table = jnp.broadcast_to(rows_table.reshape(EXPERTS, 1, capacity), (EXPERTS, 2, capacity))
    outgoing = normed_fold[dest_table.reshape(-1)]
    outgoing = outgoing.reshape(devices, pieces * capacity * folds, lanes)
    arrived = lax.all_to_all(outgoing, ("req", "z", "x"), 0, 0, tiled=True)
    sources = arrived.shape[0]
    rows = arrived.reshape(sources * capacity, folds, lanes)
    w_in = jnp.concatenate([expert_in[0, :, 0:half_units], expert_in[1, :, 0:half_units]], axis=1)
    w_in = w_in.reshape(folds, lanes, 2 * half_units)
    both_parts = jnp.einsum("tkd,kdf->tf", rows, w_in, preferred_element_type=jnp.float32)
    gate_part = both_parts[:, :half_units]
    up_part = both_parts[:, half_units:]
    inner = (jax.nn.silu(gate_part) * up_part).astype(jnp.bfloat16)
    half_out = jnp.dot(inner, expert_down, preferred_element_type=jnp.float32).astype(jnp.bfloat16)
    back = half_out.reshape(sources, capacity * folds, lanes)
    returned = lax.all_to_all(back, ("req", "z", "x"), 0, 0, tiled=True)
    slot_ids = jnp.arange(EXPERTS * capacity, dtype=jnp.int32)
    route_slots = positions.reshape(tok_local, TOP)
    mixing = jnp.sum(
        jnp.where(route_slots[:, :, None] == slot_ids[None, None, :], gate_weights[:, :, None], 0.0),
        axis=1,
    )
    mixing = jnp.broadcast_to(mixing.reshape(tok_local, EXPERTS, 1, capacity), (tok_local, EXPERTS, 2, capacity))
    mixing = mixing.reshape(tok_local, EXPERTS * 2 * capacity)
    both = returned.reshape(EXPERTS * 2 * capacity, folds, lanes).astype(jnp.float32)
    expert_out = jnp.einsum(
        "ts,skd->tkd", mixing, both, precision=lax.Precision.HIGH,
        preferred_element_type=jnp.float32,
    )
    expert_out = expert_out.astype(jnp.bfloat16).reshape(tok_local, model_width)
    return (attended, expert_out)


def solution(mesh):
    req_size, exp_size = mesh.devices.shape
    x_size = 4 if exp_size % 4 == 0 else 1
    sub_mesh = Mesh(
        mesh.devices.reshape(req_size, exp_size // x_size, x_size), ("req", "z", "x")
    )
    exp = ("z", "x")
    flat = ("req", "z", "x")
    return jax.shard_map(
        layer,
        mesh=sub_mesh,
        in_specs=(
            P("req", None, exp),
            P("req", None, None, exp),
            P("req", None, None, exp),
            P("req"),
            P(exp, None),
            P(flat, None),
            P(),
            P(flat, None),
            P(flat, None),
            P(None, None, flat),
            P(flat, None),
        ),
        out_specs=(P(flat, None), P(flat, None)),
        check_vma=False,
    )
```
